128 devices in a mesh: fsdp: 8 (over x, z_lo), dp: 16 (over z_hi, y, core).
Axes of the slice: x: 4, y: 4, z: 4 (z_hi: 2, z_lo: 2; z = z_hi * 2 + z_lo), core: 2. Of those that a mesh axis runs over, the one named last changes fastest.
Arguments:
- tokens: bfloat16 [8, 2176, 3200], P('fsdp', 'dp'), may hold values from -6 to 6
- norm_gain: float32 [3200], replicated, may hold values from 0.5 to 1.5
- qkv_weight: bfloat16 [3200, 6144], P('fsdp', 'dp'), may hold values from -4 to 4
- qk_gain: float32 [2, 2048], P(None, 'dp'), may hold values from 1 to 8
- out_weight: bfloat16 [2048, 3200], P('dp', 'fsdp'), may hold values from -0.125 to 0.125
- layer_scale: float32 [3200], replicated, may hold values from 0.2 to 1
- tile_counts: int32 [8, 2], replicated, may hold values from 0 to 2, as said below
- owners: int32 [8, 2], replicated, may hold values from 0 to 7, as said below
Outputs:
- vision_tokens: bfloat16 [32, 256, 12800], P('fsdp', None, 'dp')
The draws below stay inside these ranges and needn't reach their ends.
Inputs may be any that keep to these rules, and one draw needn't show every extreme that they name: `tile_counts`: column 0 is 1 to 2, column 1 is 0 to 2 minus column 0. All owners together get at most 4 live tiles each, and one owner gets exactly 4.
All inputs are finite; a program needn't handle non-finite values.
Results may differ from the reference program's by a relative error of at most 0.006.
The reference program's roundings to bfloat16 on the way count: a program that leaves them out, or rounds other values in their place, can miss the bound.
Values may be sent and summed in bfloat16 or wider, within the bound.
No kernel may reach another device: no remote copies, remote signals or barrier semaphores. Data moves between devices by JAX's collectives and lax.ppermute only.
A program may use at most 192 MiB of HBM per device.

```python
import math
import jax
import jax.numpy as jnp
from jax import lax

D = 3200
HEAD_DIM = 128
GRID = 32
SLOTS = 2
HEADS = 16
ROWS = 8
TILE = 1025
ROW_LEN = 2176
CAP = 4


def routing_pair(key):
    base_key = jax.random.fold_in(key, 7)
    first_key, second_key, order_key = jax.random.split(base_key, 3)
    row_index = jnp.arange(ROWS, dtype=jnp.int32)
    first_count = jax.random.randint(first_key, (ROWS,), 1, SLOTS + 1, dtype=jnp.int32)
    first_count = jnp.where(row_index < 2, SLOTS, first_count)
    second_count = jax.random.randint(second_key, (ROWS,), 0, SLOTS - first_count + 1, dtype=jnp.int32)
    counts = jnp.stack([first_count, second_count], axis=1).astype(jnp.int32)
    ordering = jax.random.permutation(order_key, ROWS).astype(jnp.int32)
    owner_first = ordering[row_index // 2]
    owner_second = ordering[ROWS // 2 + row_index // 2]
    return (counts, jnp.stack([owner_first, owner_second], axis=1).astype(jnp.int32))


def draw_tile_counts(key, part):
    return routing_pair(key)[0]


def draw_owners(key, part):
    return routing_pair(key)[1]


def draw_qkv_weight(key, part):
    standard = jnp.clip(jax.random.normal(key, (D, HEADS * 3 * HEAD_DIM), jnp.float32), -4.0, 4.0)
    column = jnp.arange(HEADS * 3 * HEAD_DIM, dtype=jnp.int32)
    head_index = (column // (3 * HEAD_DIM)).astype(jnp.float32)
    part_index = column // HEAD_DIM % 3
    position_ratio = head_index / max(HEADS - 1, 1)
    factor = 0.6 * jnp.power(3.0, position_ratio)
    factor = jnp.where(part_index < 2, factor, 1.0)
    return (standard * factor[None, :] * D ** (-0.5)).astype(jnp.bfloat16)


def draw_qk_gain(key, part):
    uniform_draw = jax.random.uniform(key, (2, HEADS * HEAD_DIM), jnp.float32)
    lower_log = jnp.log(1.0)
    upper_log = jnp.log(3.0)
    return jnp.exp(lower_log + (upper_log - lower_log) * uniform_draw)


def block_scale(key, dims, cuts, least, top_value):
    def one(dim, blocks):
        steps = jax.random.uniform(jax.random.fold_in(jax.random.fold_in(key, 6), dim), (blocks,), jnp.float32, least / len(cuts), top_value / len(cuts))
        return jnp.repeat(jnp.exp(steps), dims[dim] // blocks).reshape((-1,) + (1,) * (len(dims) - dim - 1))

    level = one(*cuts[0])
    for cut in cuts[1:]:
        level = level * one(*cut)
    return level


def normal_values(key, extent, width, most, pieces=(), kind=jnp.bfloat16):
    drawn = jax.random.normal(key, extent, jnp.float32) * width
    if len(pieces) > 0:
        drawn = block_scale(key, extent, pieces, -0.22, 0.18) * drawn
    return jnp.clip(drawn, min=-most, max=most).astype(kind)


def setup_inputs(seed: int = 0) -> dict:
    keys = jax.random.split(jax.random.key(seed), 9)
    return {
        "tokens": normal_values(keys[0], (ROWS, ROW_LEN, D), 1.0, 6.0, ((0, 8), (1, 16))),
        "norm_gain": jnp.clip(1.0 + 0.1 * jax.random.normal(keys[1], (D,), jnp.float32), 0.5, 1.5),
        "qkv_weight": draw_qkv_weight(jax.random.fold_in(keys[8], 71), 0),
        "qk_gain": draw_qk_gain(jax.random.fold_in(keys[8], 71), 0),
        "out_weight": normal_values(keys[4], (HEADS * HEAD_DIM, D), (HEADS * HEAD_DIM) ** -0.5, 0.125, ((0, 16), (1, 8))),
        "layer_scale": jnp.clip(jnp.exp(jax.random.uniform(keys[5], (D,), jnp.float32, math.log(0.2), math.log(1.0))), 0.2, 1.0),
        "tile_counts": draw_tile_counts(jax.random.fold_in(keys[8], 71), 0),
        "owners": draw_owners(jax.random.fold_in(keys[8], 71), 0),
    }


EPSILON = 1e-06

def merge_tiles(values):
    halves = GRID // 2
    columns = values.shape[1]
    tile_list = []
    for tile_slot in range(SLOTS):
        patches = values[tile_slot * TILE + 1:(tile_slot + 1) * TILE]
        square = patches.reshape(halves, 2, halves, 2, columns).transpose(0, 2, 4, 1, 3)
        tile_list.append(square.reshape(halves * halves, columns * 4))
    return jnp.stack(tile_list)

def tile_owners(tile_counts, owners):
    slot_index = jnp.arange(SLOTS, dtype=jnp.int32)[None, :]
    first_count = tile_counts[:, 0:1]
    holder = jnp.where(slot_index < first_count, owners[:, 0:1], owners[:, 1:2])
    living = slot_index < first_count + tile_counts[:, 1:2]
    return (holder, living)

def place_tiles(received, holder, living, target):
    owned_flag = jnp.logical_and(living, holder == target).reshape(-1).astype(jnp.int32)
    before = jnp.cumsum(owned_flag) - owned_flag
    chosen = jnp.logical_and(before[None, :] == jnp.arange(CAP, dtype=jnp.int32)[:, None], owned_flag[None, :] == 1)
    flattened = received.reshape(received.shape[0] * received.shape[1], -1)
    placed = jnp.dot(chosen.astype(jnp.bfloat16), flattened, preferred_element_type=jnp.float32)
    return placed.astype(jnp.bfloat16).reshape(CAP, received.shape[2], received.shape[3])

def attend_row(tokens_row, live_count, norm_gain, qkv_weight, qk_gain, out_weight, layer_scale):
    length = tokens_row.shape[0]
    model_width = tokens_row.shape[1]
    head_count = qk_gain.shape[1] // HEAD_DIM
    window = head_count * HEAD_DIM
    values = tokens_row.astype(jnp.float32)
    normed = (values * lax.rsqrt(lax.optimization_barrier(jnp.mean(values * values, axis=-1, keepdims=True)) + EPSILON) * norm_gain).astype(jnp.bfloat16)
    projected = jnp.dot(normed, qkv_weight, preferred_element_type=jnp.float32).reshape(length, head_count, 3, HEAD_DIM)
    queries = projected[:, :, 0]
    keys_part = projected[:, :, 1]
    values_part = projected[:, :, 2].astype(jnp.bfloat16)
    query_gain = qk_gain[0].reshape(head_count, HEAD_DIM)
    key_gain = qk_gain[1].reshape(head_count, HEAD_DIM)
    queries = (queries * lax.rsqrt(lax.optimization_barrier(jnp.sum(queries * queries, axis=(1, 2), keepdims=True)) / window + EPSILON) * query_gain).astype(jnp.bfloat16)
    keys_part = (keys_part * lax.rsqrt(lax.optimization_barrier(jnp.sum(keys_part * keys_part, axis=(1, 2), keepdims=True)) / window + EPSILON) * key_gain).astype(jnp.bfloat16)
    position = jnp.arange(length, dtype=jnp.int32)
    segment = jnp.minimum(position // TILE, live_count)
    same_tile = segment[:, None] == segment[None, :]
    factor = HEAD_DIM ** (-0.5)

    def head_step(running, inputs):
        query_head, key_head, value_head, weight_head = inputs
        scores = jnp.dot(query_head, key_head.T, preferred_element_type=jnp.float32) * factor
        scores = jnp.where(same_tile, scores, -1e+30)
        highest = lax.optimization_barrier(jnp.max(scores, axis=-1, keepdims=True))
        exponent = jnp.exp(scores - highest)
        weights = (exponent / lax.optimization_barrier(jnp.sum(exponent, axis=-1, keepdims=True))).astype(jnp.bfloat16)
        attended = jnp.dot(weights, value_head, preferred_element_type=jnp.float32).astype(jnp.bfloat16)
        head_term = jnp.dot(attended, weight_head, preferred_element_type=jnp.float32).astype(jnp.bfloat16)
        head_term = lax.optimization_barrier(head_term)
        return (running + head_term.astype(jnp.float32), None)
    inputs = (queries.transpose(1, 0, 2), keys_part.transpose(1, 0, 2), values_part.transpose(1, 0, 2), out_weight.reshape(head_count, HEAD_DIM, model_width))
    attention, unused = lax.scan(head_step, jnp.zeros((length, model_width), jnp.float32), inputs)
    updated = (values + layer_scale * attention).astype(jnp.bfloat16)
    return merge_tiles(updated)

def reference(tokens, norm_gain, qkv_weight, qk_gain, out_weight, layer_scale, tile_counts, owners):
    merged_rows = []
    for row_index in range(ROWS):
        live_count = (tile_counts[row_index, 0] + tile_counts[row_index, 1]).astype(jnp.int32)
        merged_rows.append(attend_row(tokens[row_index], live_count, norm_gain, qkv_weight, qk_gain, out_weight, layer_scale))
    received = jnp.stack(merged_rows)
    holder, living = tile_owners(tile_counts, owners)
    placed_list = [place_tiles(received, holder, living, target) for target in range(ROWS)]
    return jnp.concatenate(placed_list, axis=0)
```

```python
import jax
import jax.numpy as jnp
from jax import lax
from jax.sharding import PartitionSpec as P

HEAD_DIM = 128
GRID = 32
SLOTS = 2
TILE = 1025
CAP = 4


EPSILON = 1e-06


def merge_tiles(values):
    halves = GRID // 2
    columns = values.shape[1]
    tile_list = []
    for tile_slot in range(SLOTS):
        patches = values[tile_slot * TILE + 1 : (tile_slot + 1) * TILE]
        square = patches.reshape(halves, 2, halves, 2, columns).transpose(0, 2, 4, 1, 3)
        tile_list.append(square.reshape(halves * halves, columns * 4))
    return jnp.stack(tile_list)


def tile_owners(tile_counts, owners):
    slot_index = jnp.arange(SLOTS, dtype=jnp.int32)[None, :]
    first_count = tile_counts[:, 0:1]
    holder = jnp.where(slot_index < first_count, owners[:, 0:1], owners[:, 1:2])
    living = slot_index < first_count + tile_counts[:, 1:2]
    return (holder, living)


def place_tiles(received, holder, living, target):
    owned_flag = jnp.logical_and(living, holder == target).reshape(-1).astype(jnp.int32)
    before = jnp.cumsum(owned_flag) - owned_flag
    chosen = jnp.logical_and(
        before[None, :] == jnp.arange(CAP, dtype=jnp.int32)[:, None], owned_flag[None, :] == 1
    )
    flattened = received.reshape(received.shape[0] * received.shape[1], -1)
    placed = jnp.dot(chosen.astype(jnp.bfloat16), flattened, preferred_element_type=jnp.float32)
    return placed.astype(jnp.bfloat16).reshape(CAP, received.shape[2], received.shape[3])


def body(tokens, norm_gain, qkv_weight, qk_gain, out_weight, layer_scale, tile_counts, owners):
    own_rows = tokens[0]
    gathered = lax.all_gather(own_rows, "dp", axis=0, tiled=True)
    length = gathered.shape[0]
    model_width = gathered.shape[1]
    groups = lax.axis_size("dp")
    values = gathered.astype(jnp.float32)
    normed = (
        values * lax.rsqrt(jnp.mean(values * values, axis=-1, keepdims=True) + EPSILON) * norm_gain
    ).astype(jnp.bfloat16)
    projected = jnp.dot(
        normed,
        lax.all_gather(qkv_weight, "fsdp", axis=0, tiled=True),
        preferred_element_type=jnp.float32,
    )
    queries = projected[:, :HEAD_DIM]
    keys_part = projected[:, HEAD_DIM : 2 * HEAD_DIM]
    values_part = projected[:, 2 * HEAD_DIM :].astype(jnp.bfloat16)
    query_sums, key_sums = lax.psum(
        (jnp.sum(queries * queries, axis=-1), jnp.sum(keys_part * keys_part, axis=-1)), "dp"
    )
    window = groups * HEAD_DIM
    queries = (queries * lax.rsqrt(query_sums / window + EPSILON)[:, None] * qk_gain[0]).astype(
        jnp.bfloat16
    )
    keys_part = (keys_part * lax.rsqrt(key_sums / window + EPSILON)[:, None] * qk_gain[1]).astype(
        jnp.bfloat16
    )
    row_index = lax.axis_index("fsdp")
    row_count = lax.axis_size("fsdp")
    factor = HEAD_DIM ** (-0.5)
    covered = SLOTS * TILE
    tile_query = queries[:covered].reshape(SLOTS, TILE, HEAD_DIM)
    tile_key = keys_part[:covered].reshape(SLOTS, TILE, HEAD_DIM)
    tile_value = values_part[:covered].reshape(SLOTS, TILE, HEAD_DIM)
    scores = (
        jnp.einsum("sqc,skc->sqk", tile_query, tile_key, preferred_element_type=jnp.float32)
        * factor
    )
    highest = jnp.max(scores, axis=-1, keepdims=True)
    exponent = jnp.exp(scores - highest)
    weights = (exponent / jnp.sum(exponent, axis=-1, keepdims=True)).astype(jnp.bfloat16)
    tile_out = jnp.einsum(
        "sqk,skc->sqc", weights, tile_value, preferred_element_type=jnp.float32
    ).astype(jnp.bfloat16)
    head_out = jnp.concatenate(
        [
            tile_out.reshape(covered, HEAD_DIM),
            jnp.zeros((length - covered, HEAD_DIM), jnp.bfloat16),
        ],
        axis=0,
    )
    dp_index = lax.axis_index("dp")
    block = model_width // groups
    head_rows = lax.all_gather(out_weight, "fsdp", axis=1, tiled=True)
    weight_block = lax.all_to_all(head_rows, "dp", split_axis=1, concat_axis=0, tiled=True)
    all_heads = lax.all_gather(head_out, "dp", axis=0, tiled=False)
    head_terms = jnp.einsum(
        "hsc,hcd->hsd",
        all_heads,
        weight_block.reshape(groups, HEAD_DIM, block),
        preferred_element_type=jnp.float32,
    ).astype(jnp.bfloat16)
    attention = jnp.sum(lax.optimization_barrier(head_terms).astype(jnp.float32), axis=0)
    own_block = lax.dynamic_slice_in_dim(gathered, dp_index * block, block, axis=1)
    scale_block = lax.dynamic_slice_in_dim(layer_scale, dp_index * block, block)
    updated = (own_block.astype(jnp.float32) + scale_block * attention).astype(jnp.bfloat16)
    merged = merge_tiles(updated)
    holder, living = tile_owners(tile_counts, owners)
    own_holder = holder[row_index]
    own_living = living[row_index]
    destination = jnp.arange(row_count, dtype=jnp.int32)[:, None]
    sending = jnp.logical_and(destination == own_holder[None, :], own_living[None, :])
    outgoing = jnp.where(sending[:, :, None, None], merged[None], jnp.zeros((), jnp.bfloat16))
    received = lax.all_to_all(outgoing, "fsdp", split_axis=0, concat_axis=0, tiled=True)
    return place_tiles(received, holder, living, row_index)


def solution(mesh):
    placed = (
        P("fsdp", "dp", None),
        P(),
        P("fsdp", "dp"),
        P(None, "dp"),
        P("dp", "fsdp"),
        P(),
        P(),
        P(),
    )
    return jax.shard_map(
        body, mesh=mesh, in_specs=placed, out_specs=P("fsdp", None, "dp"), check_vma=False
    )
```

```python
import jax
import jax.numpy as jnp
from jax import lax
from jax.sharding import PartitionSpec as P

HEAD_DIM = 128
GRID = 32
SLOTS = 2
TILE = 1025
CAP = 4


EPSILON = 1e-06


def merge_tiles(values):
    halves = GRID // 2
    columns = values.shape[1]
    tile_list = []
    for tile_slot in range(SLOTS):
        patches = values[tile_slot * TILE + 1 : (tile_slot + 1) * TILE]
        square = patches.reshape(halves, 2, halves, 2, columns).transpose(0, 2, 4, 1, 3)
        tile_list.append(square.reshape(halves * halves, columns * 4))
    return jnp.stack(tile_list)


def tile_owners(tile_counts, owners):
    slot_index = jnp.arange(SLOTS, dtype=jnp.int32)[None, :]
    first_count = tile_counts[:, 0:1]
    holder = jnp.where(slot_index < first_count, owners[:, 0:1], owners[:, 1:2])
    living = slot_index < first_count + tile_counts[:, 1:2]
    return (holder, living)


def place_tiles(received, holder, living, target):
    owned_flag = jnp.logical_and(living, holder == target).reshape(-1).astype(jnp.int32)
    before = jnp.cumsum(owned_flag) - owned_flag
    flattened = received.reshape((received.shape[0] * received.shape[1],) + received.shape[2:])
    sources = jnp.arange(flattened.shape[0], dtype=jnp.int32)
    placed = []
    for slot in range(CAP):
        match = jnp.logical_and(before == slot, owned_flag == 1)
        source = jnp.max(jnp.where(match, sources, 0))
        tile = lax.dynamic_index_in_dim(flattened, source, axis=0, keepdims=False)
        placed.append(jnp.where(jnp.any(match), tile, jnp.zeros((), tile.dtype)))
    return jnp.stack(placed)


def gather_sum(values, axis_name, groups):
    spread = jnp.broadcast_to(values[None], (groups,) + values.shape)
    collected = lax.all_to_all(spread, axis_name, split_axis=0, concat_axis=0, tiled=True)
    return jnp.sum(collected, axis=0)


def body(tokens, norm_gain, qkv_weight, qk_gain, out_weight, layer_scale, tile_counts, owners):
    own_rows = tokens[0]
    groups = lax.axis_size("dp")
    dp_index = lax.axis_index("dp")
    model_width = own_rows.shape[1]
    block = model_width // groups
    head_rows = lax.all_gather(out_weight, "fsdp", axis=1, tiled=True)
    weight_block = lax.all_to_all(head_rows, "dp", split_axis=1, concat_axis=0, tiled=True)
    gathered = lax.all_gather(own_rows, "dp", axis=0, tiled=True)
    gathered, weight_block = lax.optimization_barrier((gathered, weight_block))
    length = gathered.shape[0]
    values = gathered.astype(jnp.float32)
    normed = (
        values * lax.rsqrt(jnp.mean(values * values, axis=-1, keepdims=True) + EPSILON) * norm_gain
    ).astype(jnp.bfloat16)
    projected = jnp.dot(
        normed,
        lax.all_gather(qkv_weight, "fsdp", axis=0, tiled=True),
        preferred_element_type=jnp.float32,
    )
    queries = projected[:, :HEAD_DIM]
    keys_part = projected[:, HEAD_DIM : 2 * HEAD_DIM]
    values_part = projected[:, 2 * HEAD_DIM :].astype(jnp.bfloat16)
    sums = gather_sum(
        jnp.stack([jnp.sum(queries * queries, axis=-1), jnp.sum(keys_part * keys_part, axis=-1)]),
        "dp",
        groups,
    )
    query_sums = sums[0]
    key_sums = sums[1]
    window = groups * HEAD_DIM
    queries = (queries * lax.rsqrt(query_sums / window + EPSILON)[:, None] * qk_gain[0]).astype(
        jnp.bfloat16
    )
    keys_part = (keys_part * lax.rsqrt(key_sums / window + EPSILON)[:, None] * qk_gain[1]).astype(
        jnp.bfloat16
    )
    row_index = lax.axis_index("fsdp")
    row_count = lax.axis_size("fsdp")
    factor = HEAD_DIM ** (-0.5)
    covered = SLOTS * TILE
    tile_query = queries[:covered].reshape(SLOTS, TILE, HEAD_DIM)
    tile_key = keys_part[:covered].reshape(SLOTS, TILE, HEAD_DIM)
    tile_value = values_part[:covered].reshape(SLOTS, TILE, HEAD_DIM)
    scores = (
        jnp.einsum("sqc,skc->sqk", tile_query, tile_key, preferred_element_type=jnp.float32)
        * factor
    )
    highest = jnp.max(scores, axis=-1, keepdims=True)
    exponent = jnp.exp(scores - highest)
    weights = (exponent / jnp.sum(exponent, axis=-1, keepdims=True)).astype(jnp.bfloat16)
    tile_out = jnp.einsum(
        "sqk,skc->sqc", weights, tile_value, preferred_element_type=jnp.float32
    ).astype(jnp.bfloat16)
    head_out = jnp.concatenate(
        [
            tile_out.reshape(covered, HEAD_DIM),
            jnp.zeros((length - covered, HEAD_DIM), jnp.bfloat16),
        ],
        axis=0,
    )
    all_heads = lax.all_gather(head_out, "dp", axis=0, tiled=False)
    head_terms = jnp.einsum(
        "hsc,hcd->hsd",
        all_heads,
        weight_block.reshape(groups, HEAD_DIM, block),
        preferred_element_type=jnp.float32,
    ).astype(jnp.bfloat16)
    attention = jnp.sum(lax.optimization_barrier(head_terms).astype(jnp.float32), axis=0)
    own_block = lax.dynamic_slice_in_dim(gathered, dp_index * block, block, axis=1)
    scale_block = lax.dynamic_slice_in_dim(layer_scale, dp_index * block, block)
    updated = (own_block.astype(jnp.float32) + scale_block * attention).astype(jnp.bfloat16)
    merged = merge_tiles(updated)
    holder, living = tile_owners(tile_counts, owners)
    own_holder = holder[row_index]
    own_living = living[row_index]
    destination = jnp.arange(row_count, dtype=jnp.int32)[:, None]
    sending = jnp.logical_and(destination == own_holder[None, :], own_living[None, :])
    outgoing = jnp.where(sending[:, :, None, None], merged[None], jnp.zeros((), jnp.bfloat16))
    received = lax.all_to_all(outgoing, "fsdp", split_axis=0, concat_axis=0, tiled=True)
    return place_tiles(received, holder, living, row_index)


def solution(mesh):
    placed = (
        P("fsdp", "dp", None),
        P(),
        P("fsdp", "dp"),
        P(None, "dp"),
        P("dp", "fsdp"),
        P(),
        P(),
        P(),
    )
    return jax.shard_map(
        body, mesh=mesh, in_specs=placed, out_specs=P("fsdp", None, "dp"), check_vma=False
    )
```

```python
import jax
import jax.numpy as jnp
from jax import lax
from jax.sharding import PartitionSpec as P

HEAD_DIM = 128
GRID = 32
SLOTS = 2
TILE = 1025
CAP = 4


EPSILON = 1e-06


def merge_tiles(values):
    halves = GRID // 2
    columns = values.shape[1]
    tile_list = []
    for tile_slot in range(SLOTS):
        patches = values[tile_slot * TILE + 1 : (tile_slot + 1) * TILE]
        square = patches.reshape(halves, 2, halves, 2, columns).transpose(0, 2, 4, 1, 3)
        tile_list.append(square.reshape(halves * halves, columns * 4))
    return jnp.stack(tile_list)


def tile_owners(tile_counts, owners):
    slot_index = jnp.arange(SLOTS, dtype=jnp.int32)[None, :]
    first_count = tile_counts[:, 0:1]
    holder = jnp.where(slot_index < first_count, owners[:, 0:1], owners[:, 1:2])
    living = slot_index < first_count + tile_counts[:, 1:2]
    return (holder, living)


def place_tiles(received, holder, living, target):
    owned_flag = jnp.logical_and(living, holder == target).reshape(-1).astype(jnp.int32)
    before = jnp.cumsum(owned_flag) - owned_flag
    flattened = received.reshape((received.shape[0] * received.shape[1],) + received.shape[2:])
    sources = jnp.arange(flattened.shape[0], dtype=jnp.int32)
    placed = []
    for slot in range(CAP):
        match = jnp.logical_and(before == slot, owned_flag == 1)
        source = jnp.max(jnp.where(match, sources, 0))
        tile = lax.dynamic_index_in_dim(flattened, source, axis=0, keepdims=False)
        placed.append(jnp.where(jnp.any(match), tile, jnp.zeros((), tile.dtype)))
    return jnp.stack(placed)


def gather_sum(values, axis_name, groups):
    spread = jnp.broadcast_to(values[None], (groups,) + values.shape)
    collected = lax.all_to_all(spread, axis_name, split_axis=0, concat_axis=0, tiled=True)
    return jnp.sum(collected, axis=0)


def gather_blocks(block_value, axis_name, groups):
    spread = jnp.broadcast_to(block_value[None], (groups,) + block_value.shape)
    collected = lax.all_to_all(spread, axis_name, split_axis=0, concat_axis=0, tiled=True)
    return collected.reshape((groups * block_value.shape[0],) + block_value.shape[1:])


def body(tokens, norm_gain, qkv_weight, qk_gain, out_weight, layer_scale, tile_counts, owners):
    own_rows = tokens[0]
    groups = lax.axis_size("dp")
    dp_index = lax.axis_index("dp")
    row_index = lax.axis_index("fsdp")
    row_count = lax.axis_size("fsdp")
    model_width = own_rows.shape[1]
    block = model_width // groups
    head_rows = lax.all_gather(out_weight, "fsdp", axis=1, tiled=True)
    weight_block = lax.all_to_all(head_rows, "dp", split_axis=1, concat_axis=0, tiled=True)
    full_qkv = gather_blocks(qkv_weight, "fsdp", row_count)
    full_qkv, weight_block = lax.optimization_barrier((full_qkv, weight_block))
    gathered = lax.all_gather(own_rows, "dp", axis=0, tiled=True)
    values = gathered.astype(jnp.float32)
    normed = (
        values * lax.rsqrt(jnp.mean(values * values, axis=-1, keepdims=True) + EPSILON) * norm_gain
    ).astype(jnp.bfloat16)
    projected = jnp.dot(normed, full_qkv, preferred_element_type=jnp.float32)
    queries = projected[:, :HEAD_DIM]
    keys_part = projected[:, HEAD_DIM : 2 * HEAD_DIM]
    values_part = projected[:, 2 * HEAD_DIM :].astype(jnp.bfloat16)
    sums = gather_sum(
        jnp.stack([jnp.sum(queries * queries, axis=-1), jnp.sum(keys_part * keys_part, axis=-1)]),
        "dp",
        groups,
    )
    window = groups * HEAD_DIM
    queries = (queries * lax.rsqrt(sums[0] / window + EPSILON)[:, None] * qk_gain[0]).astype(
        jnp.bfloat16
    )
    keys_part = (keys_part * lax.rsqrt(sums[1] / window + EPSILON)[:, None] * qk_gain[1]).astype(
        jnp.bfloat16
    )
    factor = HEAD_DIM ** (-0.5)
    own_block = lax.dynamic_slice_in_dim(gathered, dp_index * block, block, axis=1)
    scale_block = lax.dynamic_slice_in_dim(layer_scale, dp_index * block, block)
    holder, living = tile_owners(tile_counts, owners)
    own_holder = holder[row_index]
    own_living = living[row_index]
    destination = jnp.arange(row_count, dtype=jnp.int32)[:, None]
    sending = jnp.logical_and(destination == own_holder[None, :], own_living[None, :])
    halves = GRID // 2
    slot_received = []
    for tile_slot in range(SLOTS):
        first = tile_slot * TILE
        tile_query = queries[first : first + TILE]
        tile_key = keys_part[first : first + TILE]
        tile_value = values_part[first : first + TILE]
        scores = jnp.dot(tile_query[1:], tile_key.T, preferred_element_type=jnp.float32) * factor
        highest = jnp.max(scores, axis=-1, keepdims=True)
        exponent = jnp.exp(scores - highest)
        weights = (exponent / jnp.sum(exponent, axis=-1, keepdims=True)).astype(jnp.bfloat16)
        tile_out = jnp.dot(weights, tile_value, preferred_element_type=jnp.float32).astype(
            jnp.bfloat16
        )
        all_heads = lax.all_gather(tile_out, "dp", axis=0, tiled=False)
        head_terms = jnp.einsum(
            "hsc,hcd->hsd",
            all_heads,
            weight_block.reshape(groups, HEAD_DIM, block),
            preferred_element_type=jnp.float32,
        ).astype(jnp.bfloat16)
        attention = jnp.sum(lax.optimization_barrier(head_terms).astype(jnp.float32), axis=0)
        patches = own_block[first + 1 : first + TILE]
        updated = (patches.astype(jnp.float32) + scale_block * attention).astype(jnp.bfloat16)
        square = updated.reshape(halves, 2, halves, 2, block).transpose(0, 2, 4, 1, 3)
        merged = square.reshape(halves * halves, block * 4)
        outgoing = jnp.where(
            sending[:, tile_slot, None, None], merged[None], jnp.zeros((), jnp.bfloat16)
        )
        slot_received.append(
            lax.all_to_all(outgoing, "fsdp", split_axis=0, concat_axis=0, tiled=True)
        )
    received = jnp.stack(slot_received, axis=1)
    return place_tiles(received, holder, living, row_index)


def solution(mesh):
    placed = (
        P("fsdp", "dp", None),
        P(),
        P("fsdp", "dp"),
        P(None, "dp"),
        P("dp", "fsdp"),
        P(),
        P(),
        P(),
    )
    return jax.shard_map(
        body, mesh=mesh, in_specs=placed, out_specs=P("fsdp", None, "dp"), check_vma=False
    )
```

```python
import jax
import jax.numpy as jnp
from jax import lax
from jax.sharding import PartitionSpec as P

HEAD_DIM = 128
GRID = 32
SLOTS = 2
TILE = 1025
CAP = 4


EPSILON = 1e-06


def merge_tiles(values):
    halves = GRID // 2
    columns = values.shape[1]
    tile_list = []
    for tile_slot in range(SLOTS):
        patches = values[tile_slot * TILE + 1 : (tile_slot + 1) * TILE]
        square = patches.reshape(halves, 2, halves, 2, columns).transpose(0, 2, 4, 1, 3)
        tile_list.append(square.reshape(halves * halves, columns * 4))
    return jnp.stack(tile_list)


def tile_owners(tile_counts, owners):
    slot_index = jnp.arange(SLOTS, dtype=jnp.int32)[None, :]
    first_count = tile_counts[:, 0:1]
    holder = jnp.where(slot_index < first_count, owners[:, 0:1], owners[:, 1:2])
    living = slot_index < first_count + tile_counts[:, 1:2]
    return (holder, living)


def place_tiles(received, holder, living, target):
    owned_flag = jnp.logical_and(living, holder == target).reshape(-1).astype(jnp.int32)
    before = jnp.cumsum(owned_flag) - owned_flag
    flattened = received.reshape((received.shape[0] * received.shape[1],) + received.shape[2:])
    sources = jnp.arange(flattened.shape[0], dtype=jnp.int32)
    placed = []
    for slot in range(CAP):
        match = jnp.logical_and(before == slot, owned_flag == 1)
        source = jnp.max(jnp.where(match, sources, 0))
        tile = lax.dynamic_index_in_dim(flattened, source, axis=0, keepdims=False)
        placed.append(jnp.where(jnp.any(match), tile, jnp.zeros((), tile.dtype)))
    return jnp.stack(placed)


def gather_sum(values, axis_name, groups):
    spread = jnp.broadcast_to(values[None], (groups,) + values.shape)
    collected = lax.all_to_all(spread, axis_name, split_axis=0, concat_axis=0, tiled=True)
    return jnp.sum(collected, axis=0)


def gather_blocks(block_value, axis_name, groups):
    spread = jnp.broadcast_to(block_value[None], (groups,) + block_value.shape)
    collected = lax.all_to_all(spread, axis_name, split_axis=0, concat_axis=0, tiled=True)
    return collected.reshape((groups * block_value.shape[0],) + block_value.shape[1:])


def body(tokens, norm_gain, qkv_weight, qk_gain, out_weight, layer_scale, tile_counts, owners):
    own_rows = tokens[0]
    groups = lax.axis_size("dp")
    dp_index = lax.axis_index("dp")
    row_index = lax.axis_index("fsdp")
    row_count = lax.axis_size("fsdp")
    model_width = own_rows.shape[1]
    block = model_width // groups
    head_rows = lax.all_gather(out_weight, "fsdp", axis=1, tiled=True)
    weight_block = lax.all_to_all(head_rows, "dp", split_axis=1, concat_axis=0, tiled=True)
    full_qkv = gather_blocks(qkv_weight, "fsdp", row_count)
    full_qkv, weight_block = lax.optimization_barrier((full_qkv, weight_block))
    gathered = lax.all_gather(own_rows, "dp", axis=0, tiled=True)
    values = gathered.astype(jnp.float32)
    normed = (
        values * lax.rsqrt(jnp.mean(values * values, axis=-1, keepdims=True) + EPSILON) * norm_gain
    ).astype(jnp.bfloat16)
    projected = jnp.dot(normed, full_qkv, preferred_element_type=jnp.float32)
    queries = projected[:, :HEAD_DIM]
    keys_part = projected[:, HEAD_DIM : 2 * HEAD_DIM]
    values_part = projected[:, 2 * HEAD_DIM :].astype(jnp.bfloat16)
    sums = gather_sum(
        jnp.stack([jnp.sum(queries * queries, axis=-1), jnp.sum(keys_part * keys_part, axis=-1)]),
        "dp",
        groups,
    )
    window = groups * HEAD_DIM
    queries = (queries * lax.rsqrt(sums[0] / window + EPSILON)[:, None] * qk_gain[0]).astype(
        jnp.bfloat16
    )
    keys_part = (keys_part * lax.rsqrt(sums[1] / window + EPSILON)[:, None] * qk_gain[1]).astype(
        jnp.bfloat16
    )
    factor = HEAD_DIM ** (-0.5)
    own_block = lax.dynamic_slice_in_dim(gathered, dp_index * block, block, axis=1)
    scale_block = lax.dynamic_slice_in_dim(layer_scale, dp_index * block, block)
    holder, living = tile_owners(tile_counts, owners)
    own_holder = holder[row_index]
    own_living = living[row_index]
    destination = jnp.arange(row_count, dtype=jnp.int32)[:, None]
    sending = jnp.logical_and(destination == own_holder[None, :], own_living[None, :])
    halves = GRID // 2
    slot_received = []
    for tile_slot in range(SLOTS):
        first = tile_slot * TILE
        tile_query = queries[first : first + TILE]
        tile_key = keys_part[first : first + TILE]
        tile_value = values_part[first : first + TILE]
        scores = jnp.dot(tile_query[1:], tile_key.T, preferred_element_type=jnp.float32) * factor
        highest = jnp.max(scores, axis=-1, keepdims=True)
        exponent = jnp.exp(scores - highest)
        weights = (exponent / jnp.sum(exponent, axis=-1, keepdims=True)).astype(jnp.bfloat16)
        tile_out = jnp.dot(weights, tile_value, preferred_element_type=jnp.float32).astype(
            jnp.bfloat16
        )
        all_heads = lax.all_gather(tile_out, "dp", axis=0, tiled=False)
        if slot_received:
            all_heads, slot_received[-1] = lax.optimization_barrier((all_heads, slot_received[-1]))
        head_terms = jnp.einsum(
            "hsc,hcd->hsd",
            all_heads,
            weight_block.reshape(groups, HEAD_DIM, block),
            preferred_element_type=jnp.float32,
        ).astype(jnp.bfloat16)
        attention = jnp.sum(lax.optimization_barrier(head_terms).astype(jnp.float32), axis=0)
        patches = own_block[first + 1 : first + TILE]
        updated = (patches.astype(jnp.float32) + scale_block * attention).astype(jnp.bfloat16)
        square = updated.reshape(halves, 2, halves, 2, block).transpose(0, 2, 4, 1, 3)
        merged = square.reshape(halves * halves, block * 4)
        outgoing = jnp.where(
            sending[:, tile_slot, None, None], merged[None], jnp.zeros((), jnp.bfloat16)
        )
        slot_received.append(
            lax.all_to_all(outgoing, "fsdp", split_axis=0, concat_axis=0, tiled=True)
        )
    received = jnp.stack(slot_received, axis=1)
    return place_tiles(received, holder, living, row_index)


def solution(mesh):
    placed = (
        P("fsdp", "dp", None),
        P(),
        P("fsdp", "dp"),
        P(None, "dp"),
        P("dp", "fsdp"),
        P(),
        P(),
        P(),
    )
    return jax.shard_map(
        body, mesh=mesh, in_specs=placed, out_specs=P("fsdp", None, "dp"), check_vma=False
    )
```

```python
import jax
import jax.numpy as jnp
from jax import lax
from jax.sharding import Mesh, PartitionSpec as P

HEAD_DIM = 128
GRID = 32
SLOTS = 2
TILE = 1025
CAP = 4


EPSILON = 1e-06


def merge_tiles(values):
    halves = GRID // 2
    columns = values.shape[1]
    tile_list = []
    for tile_slot in range(SLOTS):
        patches = values[tile_slot * TILE + 1 : (tile_slot + 1) * TILE]
        square = patches.reshape(halves, 2, halves, 2, columns).transpose(0, 2, 4, 1, 3)
        tile_list.append(square.reshape(halves * halves, columns * 4))
    return jnp.stack(tile_list)


def tile_owners(tile_counts, owners):
    slot_index = jnp.arange(SLOTS, dtype=jnp.int32)[None, :]
    first_count = tile_counts[:, 0:1]
    holder = jnp.where(slot_index < first_count, owners[:, 0:1], owners[:, 1:2])
    living = slot_index < first_count + tile_counts[:, 1:2]
    return (holder, living)


def place_tiles(received, holder, living, target):
    owned_flag = jnp.logical_and(living, holder == target).reshape(-1).astype(jnp.int32)
    before = jnp.cumsum(owned_flag) - owned_flag
    flattened = received.reshape((received.shape[0] * received.shape[1],) + received.shape[2:])
    sources = jnp.arange(flattened.shape[0], dtype=jnp.int32)
    placed = []
    for slot in range(CAP):
        match = jnp.logical_and(before == slot, owned_flag == 1)
        source = jnp.max(jnp.where(match, sources, 0))
        tile = lax.dynamic_index_in_dim(flattened, source, axis=0, keepdims=False)
        placed.append(jnp.where(jnp.any(match), tile, jnp.zeros((), tile.dtype)))
    return jnp.stack(placed)


def gather_sum(values, axis_name, groups):
    spread = jnp.broadcast_to(values[None], (groups,) + values.shape)
    collected = lax.all_to_all(spread, axis_name, split_axis=0, concat_axis=0, tiled=True)
    return jnp.sum(collected, axis=0)


def gather_blocks(block_value, axis_name, groups):
    spread = jnp.broadcast_to(block_value[None], (groups,) + block_value.shape)
    collected = lax.all_to_all(spread, axis_name, split_axis=0, concat_axis=0, tiled=True)
    return collected.reshape((groups * block_value.shape[0],) + block_value.shape[1:])


def body(tokens, norm_gain, qkv_weight, qk_gain, out_weight, layer_scale, tile_counts, owners):
    own_rows = tokens[0]
    chips = lax.axis_size("chip")
    cores = lax.axis_size("core")
    groups = chips * cores
    chip = lax.axis_index("chip")
    core = lax.axis_index("core")
    row_index = lax.axis_index("fsdp")
    row_count = lax.axis_size("fsdp")
    model_width = own_rows.shape[1]
    block = model_width // groups
    swap = [(0, 1), (1, 0)]
    head_rows = lax.all_gather(out_weight, "fsdp", axis=1, tiled=True)
    weight_block = lax.all_to_all(
        head_rows, ("chip", "core"), split_axis=1, concat_axis=0, tiled=True
    )
    pair_weight = lax.all_gather(weight_block, "core", axis=1, tiled=True)
    full_qkv = gather_blocks(qkv_weight, "fsdp", row_count)
    pair_qkv = lax.all_gather(full_qkv, "core", axis=1, tiled=True)
    pair_qkv, pair_weight = lax.optimization_barrier((pair_qkv, pair_weight))
    pair_gain = lax.all_gather(qk_gain, "core", axis=1, tiled=True).reshape(2, cores, HEAD_DIM)
    half = lax.all_gather(own_rows, "chip", axis=0, tiled=True)
    half_length = half.shape[0]
    piece = own_rows.shape[0]
    values = half.astype(jnp.float32)
    normed = (
        values * lax.rsqrt(jnp.mean(values * values, axis=-1, keepdims=True) + EPSILON) * norm_gain
    ).astype(jnp.bfloat16)
    projected = jnp.dot(normed, pair_qkv, preferred_element_type=jnp.float32)
    projected = projected.reshape(half_length, cores, 3, HEAD_DIM)
    queries = projected[:, :, 0]
    keys_part = projected[:, :, 1]
    values_part = projected[:, :, 2].astype(jnp.bfloat16)
    sums = gather_sum(
        jnp.stack(
            [jnp.sum(queries * queries, axis=(1, 2)), jnp.sum(keys_part * keys_part, axis=(1, 2))]
        ),
        "chip",
        chips,
    )
    window = groups * HEAD_DIM
    queries = (
        queries * lax.rsqrt(sums[0] / window + EPSILON)[:, None, None] * pair_gain[0][None]
    ).astype(jnp.bfloat16)
    keys_part = (
        keys_part * lax.rsqrt(sums[1] / window + EPSILON)[:, None, None] * pair_gain[1][None]
    ).astype(jnp.bfloat16)
    stacked = jnp.stack([queries, keys_part, values_part])
    mine = lax.dynamic_index_in_dim(stacked, core, axis=2, keepdims=False)
    theirs = lax.dynamic_index_in_dim(stacked, 1 - core, axis=2, keepdims=False)
    got = lax.ppermute(theirs, "core", swap)
    first_half = jnp.where(core == 0, mine, got).reshape(3, chips, piece, HEAD_DIM)
    second_half = jnp.where(core == 0, got, mine).reshape(3, chips, piece, HEAD_DIM)
    whole = jnp.stack([first_half, second_half], axis=2).reshape(3, groups * piece, HEAD_DIM)
    length = whole.shape[1]
    factor = HEAD_DIM ** (-0.5)
    covered = SLOTS * TILE
    tile_query = whole[0, :covered].reshape(SLOTS, TILE, HEAD_DIM)
    tile_key = whole[1, :covered].reshape(SLOTS, TILE, HEAD_DIM)
    tile_value = whole[2, :covered].reshape(SLOTS, TILE, HEAD_DIM)
    scores = (
        jnp.einsum("sqc,skc->sqk", tile_query, tile_key, preferred_element_type=jnp.float32)
        * factor
    )
    highest = jnp.max(scores, axis=-1, keepdims=True)
    exponent = jnp.exp(scores - highest)
    weights = (exponent / jnp.sum(exponent, axis=-1, keepdims=True)).astype(jnp.bfloat16)
    tile_out = jnp.einsum(
        "sqk,skc->sqc", weights, tile_value, preferred_element_type=jnp.float32
    ).astype(jnp.bfloat16)
    head_out = jnp.concatenate(
        [
            tile_out.reshape(covered, HEAD_DIM),
            jnp.zeros((length - covered, HEAD_DIM), jnp.bfloat16),
        ],
        axis=0,
    )
    by_half = head_out.reshape(chips, cores, piece, HEAD_DIM).transpose(1, 0, 2, 3)
    by_half = by_half.reshape(cores, half_length, HEAD_DIM)
    outgoing = jnp.broadcast_to(by_half[None], (chips, cores, half_length, HEAD_DIM))
    all_heads = lax.all_to_all(
        outgoing.reshape(groups, half_length, HEAD_DIM),
        ("chip", "core"),
        split_axis=0,
        concat_axis=0,
        tiled=True,
    )
    head_terms = jnp.einsum(
        "hsc,hcd->hsd",
        all_heads,
        pair_weight.reshape(groups, HEAD_DIM, cores * block),
        preferred_element_type=jnp.float32,
    ).astype(jnp.bfloat16)
    attention = jnp.sum(lax.optimization_barrier(head_terms).astype(jnp.float32), axis=0)
    pair_tokens = lax.dynamic_slice_in_dim(half, chip * cores * block, cores * block, axis=1)
    pair_scale = lax.dynamic_slice_in_dim(layer_scale, chip * cores * block, cores * block)
    updated_half = (pair_tokens.astype(jnp.float32) + pair_scale * attention).astype(jnp.bfloat16)
    keep = lax.dynamic_slice_in_dim(updated_half, core * block, block, axis=1)
    give = lax.dynamic_slice_in_dim(updated_half, (1 - core) * block, block, axis=1)
    taken = lax.ppermute(give, "core", swap)
    first_half = jnp.where(core == 0, keep, taken).reshape(chips, piece, block)
    second_half = jnp.where(core == 0, taken, keep).reshape(chips, piece, block)
    updated = jnp.stack([first_half, second_half], axis=1).reshape(length, block)
    merged = merge_tiles(updated)
    holder, living = tile_owners(tile_counts, owners)
    own_holder = holder[row_index]
    own_living = living[row_index]
    destination = jnp.arange(row_count, dtype=jnp.int32)[:, None]
    sending = jnp.logical_and(destination == own_holder[None, :], own_living[None, :])
    outgoing = jnp.where(sending[:, :, None, None], merged[None], jnp.zeros((), jnp.bfloat16))
    received = lax.all_to_all(outgoing, "fsdp", split_axis=0, concat_axis=0, tiled=True)
    return place_tiles(received, holder, living, row_index)


def solution(mesh):
    fsdp_size = mesh.shape["fsdp"]
    dp_size = mesh.shape["dp"]
    split = Mesh(
        mesh.devices.reshape(fsdp_size, dp_size // 2, 2), ("fsdp", "chip", "core")
    )
    heads = ("chip", "core")
    placed = (
        P("fsdp", heads, None),
        P(),
        P("fsdp", heads),
        P(None, heads),
        P(heads, "fsdp"),
        P(),
        P(),
        P(),
    )
    return jax.shard_map(
        body, mesh=split, in_specs=placed, out_specs=P("fsdp", None, heads), check_vma=False
    )
```

```python
import jax
import jax.numpy as jnp
from jax import lax
from jax.sharding import Mesh, PartitionSpec as P

HEAD_DIM = 128
GRID = 32
SLOTS = 2
TILE = 1025
CAP = 4


EPSILON = 1e-06


def merge_tiles(values):
    halves = GRID // 2
    columns = values.shape[1]
    tile_list = []
    for tile_slot in range(SLOTS):
        patches = values[tile_slot * TILE + 1 : (tile_slot + 1) * TILE]
        square = patches.reshape(halves, 2, halves, 2, columns).transpose(0, 2, 4, 1, 3)
        tile_list.append(square.reshape(halves * halves, columns * 4))
    return jnp.stack(tile_list)


def tile_owners(tile_counts, owners):
    slot_index = jnp.arange(SLOTS, dtype=jnp.int32)[None, :]
    first_count = tile_counts[:, 0:1]
    holder = jnp.where(slot_index < first_count, owners[:, 0:1], owners[:, 1:2])
    living = slot_index < first_count + tile_counts[:, 1:2]
    return (holder, living)


def place_tiles(received, holder, living, target):
    owned_flag = jnp.logical_and(living, holder == target).reshape(-1).astype(jnp.int32)
    before = jnp.cumsum(owned_flag) - owned_flag
    flattened = received.reshape((received.shape[0] * received.shape[1],) + received.shape[2:])
    sources = jnp.arange(flattened.shape[0], dtype=jnp.int32)
    placed = []
    for slot in range(CAP):
        match = jnp.logical_and(before == slot, owned_flag == 1)
        source = jnp.max(jnp.where(match, sources, 0))
        tile = lax.dynamic_index_in_dim(flattened, source, axis=0, keepdims=False)
        placed.append(jnp.where(jnp.any(match), tile, jnp.zeros((), tile.dtype)))
    return jnp.stack(placed)


def gather_sum(values, axis_name, groups):
    spread = jnp.broadcast_to(values[None], (groups,) + values.shape)
    collected = lax.all_to_all(spread, axis_name, split_axis=0, concat_axis=0, tiled=True)
    return jnp.sum(collected, axis=0)


def gather_blocks(block_value, axis_name, groups):
    spread = jnp.broadcast_to(block_value[None], (groups,) + block_value.shape)
    collected = lax.all_to_all(spread, axis_name, split_axis=0, concat_axis=0, tiled=True)
    return collected.reshape((groups * block_value.shape[0],) + block_value.shape[1:])


def pair_up(value, core, swap, axis):
    other = lax.ppermute(value, "core", swap)
    low = jnp.where(core == 0, value, other)
    high = jnp.where(core == 0, other, value)
    return jnp.concatenate([low, high], axis=axis)


def body(tokens, norm_gain, qkv_weight, qk_gain, out_weight, layer_scale, tile_counts, owners):
    own_rows = tokens[0]
    chips = lax.axis_size("chip")
    cores = lax.axis_size("core")
    groups = chips * cores
    chip = lax.axis_index("chip")
    core = lax.axis_index("core")
    row_index = lax.axis_index("fsdp")
    row_count = lax.axis_size("fsdp")
    model_width = own_rows.shape[1]
    block = model_width // groups
    swap = [(0, 1), (1, 0)]
    head_rows = lax.all_gather(out_weight, "fsdp", axis=1, tiled=True)
    weight_block = lax.all_to_all(
        head_rows, ("chip", "core"), split_axis=1, concat_axis=0, tiled=True
    )
    pair_weight = pair_up(weight_block, core, swap, 1)
    full_qkv = gather_blocks(qkv_weight, "fsdp", row_count)
    pair_qkv = pair_up(full_qkv, core, swap, 1)
    pair_qkv, pair_weight = lax.optimization_barrier((pair_qkv, pair_weight))
    pair_gain = pair_up(qk_gain, core, swap, 1).reshape(2, cores, HEAD_DIM)
    half = lax.all_gather(own_rows, "chip", axis=0, tiled=True)
    half_length = half.shape[0]
    piece = own_rows.shape[0]
    values = half.astype(jnp.float32)
    normed = (
        values * lax.rsqrt(jnp.mean(values * values, axis=-1, keepdims=True) + EPSILON) * norm_gain
    ).astype(jnp.bfloat16)
    projected = jnp.dot(normed, pair_qkv, preferred_element_type=jnp.float32)
    projected = projected.reshape(half_length, cores, 3, HEAD_DIM)
    queries = projected[:, :, 0]
    keys_part = projected[:, :, 1]
    values_part = projected[:, :, 2].astype(jnp.bfloat16)
    sums = gather_sum(
        jnp.stack(
            [jnp.sum(queries * queries, axis=(1, 2)), jnp.sum(keys_part * keys_part, axis=(1, 2))]
        ),
        "chip",
        chips,
    )
    window = groups * HEAD_DIM
    queries = (
        queries * lax.rsqrt(sums[0] / window + EPSILON)[:, None, None] * pair_gain[0][None]
    ).astype(jnp.bfloat16)
    keys_part = (
        keys_part * lax.rsqrt(sums[1] / window + EPSILON)[:, None, None] * pair_gain[1][None]
    ).astype(jnp.bfloat16)
    stacked = jnp.stack([queries, keys_part, values_part])
    mine = lax.dynamic_index_in_dim(stacked, core, axis=2, keepdims=False)
    theirs = lax.dynamic_index_in_dim(stacked, 1 - core, axis=2, keepdims=False)
    got = lax.ppermute(theirs, "core", swap)
    first_half = jnp.where(core == 0, mine, got).reshape(3, chips, piece, HEAD_DIM)
    second_half = jnp.where(core == 0, got, mine).reshape(3, chips, piece, HEAD_DIM)
    whole = jnp.stack([first_half, second_half], axis=2).reshape(3, groups * piece, HEAD_DIM)
    length = whole.shape[1]
    factor = HEAD_DIM ** (-0.5)
    covered = SLOTS * TILE
    tile_query = whole[0, :covered].reshape(SLOTS, TILE, HEAD_DIM)
    tile_key = whole[1, :covered].reshape(SLOTS, TILE, HEAD_DIM)
    tile_value = whole[2, :covered].reshape(SLOTS, TILE, HEAD_DIM)
    scores = (
        jnp.einsum("sqc,skc->sqk", tile_query, tile_key, preferred_element_type=jnp.float32)
        * factor
    )
    highest = jnp.max(scores, axis=-1, keepdims=True)
    exponent = jnp.exp(scores - highest)
    weights = (exponent / jnp.sum(exponent, axis=-1, keepdims=True)).astype(jnp.bfloat16)
    tile_out = jnp.einsum(
        "sqk,skc->sqc", weights, tile_value, preferred_element_type=jnp.float32
    ).astype(jnp.bfloat16)
    head_out = jnp.concatenate(
        [
            tile_out.reshape(covered, HEAD_DIM),
            jnp.zeros((length - covered, HEAD_DIM), jnp.bfloat16),
        ],
        axis=0,
    )
    by_half = head_out.reshape(chips, cores, piece, HEAD_DIM).transpose(1, 0, 2, 3)
    by_half = by_half.reshape(cores, half_length, HEAD_DIM)
    outgoing = jnp.broadcast_to(by_half[None], (chips, cores, half_length, HEAD_DIM))
    all_heads = lax.all_to_all(
        outgoing.reshape(groups, half_length, HEAD_DIM),
        ("chip", "core"),
        split_axis=0,
        concat_axis=0,
        tiled=True,
    )
    head_terms = jnp.einsum(
        "hsc,hcd->hsd",
        all_heads,
        pair_weight.reshape(groups, HEAD_DIM, cores * block),
        preferred_element_type=jnp.float32,
    ).astype(jnp.bfloat16)
    attention = jnp.sum(lax.optimization_barrier(head_terms).astype(jnp.float32), axis=0)
    pair_tokens = lax.dynamic_slice_in_dim(half, chip * cores * block, cores * block, axis=1)
    pair_scale = lax.dynamic_slice_in_dim(layer_scale, chip * cores * block, cores * block)
    updated_half = (pair_tokens.astype(jnp.float32) + pair_scale * attention).astype(jnp.bfloat16)
    keep = lax.dynamic_slice_in_dim(updated_half, core * block, block, axis=1)
    give = lax.dynamic_slice_in_dim(updated_half, (1 - core) * block, block, axis=1)
    taken = lax.ppermute(give, "core", swap)
    first_half = jnp.where(core == 0, keep, taken).reshape(chips, piece, block)
    second_half = jnp.where(core == 0, taken, keep).reshape(chips, piece, block)
    updated = jnp.stack([first_half, second_half], axis=1).reshape(length, block)
    merged = merge_tiles(updated)
    holder, living = tile_owners(tile_counts, owners)
    own_holder = holder[row_index]
    own_living = living[row_index]
    destination = jnp.arange(row_count, dtype=jnp.int32)[:, None]
    sending = jnp.logical_and(destination == own_holder[None, :], own_living[None, :])
    outgoing = jnp.where(sending[:, :, None, None], merged[None], jnp.zeros((), jnp.bfloat16))
    received = lax.all_to_all(outgoing, "fsdp", split_axis=0, concat_axis=0, tiled=True)
    return place_tiles(received, holder, living, row_index)


def solution(mesh):
    fsdp_size = mesh.shape["fsdp"]
    dp_size = mesh.shape["dp"]
    split = Mesh(
        mesh.devices.reshape(fsdp_size, dp_size // 2, 2), ("fsdp", "chip", "core")
    )
    heads = ("chip", "core")
    placed = (
        P("fsdp", heads, None),
        P(),
        P("fsdp", heads),
        P(None, heads),
        P(heads, "fsdp"),
        P(),
        P(),
        P(),
    )
    return jax.shard_map(
        body, mesh=split, in_specs=placed, out_specs=P("fsdp", None, heads), check_vma=False
    )
```

```python
import jax
import jax.numpy as jnp
from jax import lax
from jax.sharding import Mesh, PartitionSpec as P

HEAD_DIM = 128
GRID = 32
SLOTS = 2
TILE = 1025
CAP = 4


EPSILON = 1e-06


def merge_tiles(values):
    halves = GRID // 2
    columns = values.shape[1]
    tile_list = []
    for tile_slot in range(SLOTS):
        patches = values[tile_slot * TILE + 1 : (tile_slot + 1) * TILE]
        square = patches.reshape(halves, 2, halves, 2, columns).transpose(0, 2, 4, 1, 3)
        tile_list.append(square.reshape(halves * halves, columns * 4))
    return jnp.stack(tile_list)


def merge_one(patches):
    halves = GRID // 2
    columns = patches.shape[1]
    square = patches.reshape(halves, 2, halves, 2, columns).transpose(0, 2, 4, 1, 3)
    return square.reshape(halves * halves, columns * 4)


def tile_owners(tile_counts, owners):
    slot_index = jnp.arange(SLOTS, dtype=jnp.int32)[None, :]
    first_count = tile_counts[:, 0:1]
    holder = jnp.where(slot_index < first_count, owners[:, 0:1], owners[:, 1:2])
    living = slot_index < first_count + tile_counts[:, 1:2]
    return (holder, living)


def place_tiles(received, holder, living, target):
    owned_flag = jnp.logical_and(living, holder == target).reshape(-1).astype(jnp.int32)
    before = jnp.cumsum(owned_flag) - owned_flag
    flattened = received.reshape((received.shape[0] * received.shape[1],) + received.shape[2:])
    sources = jnp.arange(flattened.shape[0], dtype=jnp.int32)
    placed = []
    for slot in range(CAP):
        match = jnp.logical_and(before == slot, owned_flag == 1)
        source = jnp.max(jnp.where(match, sources, 0))
        tile = lax.dynamic_index_in_dim(flattened, source, axis=0, keepdims=False)
        placed.append(jnp.where(jnp.any(match), tile, jnp.zeros((), tile.dtype)))
    return jnp.stack(placed)


def gather_sum(values, axis_name, groups):
    spread = jnp.broadcast_to(values[None], (groups,) + values.shape)
    collected = lax.all_to_all(spread, axis_name, split_axis=0, concat_axis=0, tiled=True)
    return jnp.sum(collected, axis=0)


def gather_blocks(block_value, axis_name, groups):
    spread = jnp.broadcast_to(block_value[None], (groups,) + block_value.shape)
    collected = lax.all_to_all(spread, axis_name, split_axis=0, concat_axis=0, tiled=True)
    return collected.reshape((groups * block_value.shape[0],) + block_value.shape[1:])


def pair_up(value, core, swap, axis):
    other = lax.ppermute(value, "core", swap)
    low = jnp.where(core == 0, value, other)
    high = jnp.where(core == 0, other, value)
    return jnp.concatenate([low, high], axis=axis)


def body(tokens, norm_gain, qkv_weight, qk_gain, out_weight, layer_scale, tile_counts, owners):
    own_rows = tokens[0]
    chips = lax.axis_size("chip")
    cores = lax.axis_size("core")
    groups = chips * cores
    chip = lax.axis_index("chip")
    core = lax.axis_index("core")
    row_index = lax.axis_index("fsdp")
    row_count = lax.axis_size("fsdp")
    model_width = own_rows.shape[1]
    block = model_width // groups
    swap = [(0, 1), (1, 0)]
    head_rows = lax.all_gather(out_weight, "fsdp", axis=1, tiled=True)
    weight_block = lax.all_to_all(
        head_rows, ("chip", "core"), split_axis=1, concat_axis=0, tiled=True
    )
    pair_weight = pair_up(weight_block, core, swap, 1)
    full_qkv = gather_blocks(qkv_weight, "fsdp", row_count)
    pair_qkv = pair_up(full_qkv, core, swap, 1)
    pair_qkv, pair_weight = lax.optimization_barrier((pair_qkv, pair_weight))
    pair_gain = pair_up(qk_gain, core, swap, 1).reshape(2, cores, HEAD_DIM)
    half = lax.all_gather(own_rows, "chip", axis=0, tiled=True)
    half_length = half.shape[0]
    piece = own_rows.shape[0]
    values = half.astype(jnp.float32)
    normed = (
        values * lax.rsqrt(jnp.mean(values * values, axis=-1, keepdims=True) + EPSILON) * norm_gain
    ).astype(jnp.bfloat16)
    projected = jnp.dot(normed, pair_qkv, preferred_element_type=jnp.float32)
    projected = projected.reshape(half_length, cores, 3, HEAD_DIM)
    queries = projected[:, :, 0]
    keys_part = projected[:, :, 1]
    values_part = projected[:, :, 2].astype(jnp.bfloat16)
    sums = gather_sum(
        jnp.stack(
            [jnp.sum(queries * queries, axis=(1, 2)), jnp.sum(keys_part * keys_part, axis=(1, 2))]
        ),
        "chip",
        chips,
    )
    window = groups * HEAD_DIM
    queries = (
        queries * lax.rsqrt(sums[0] / window + EPSILON)[:, None, None] * pair_gain[0][None]
    ).astype(jnp.bfloat16)
    keys_part = (
        keys_part * lax.rsqrt(sums[1] / window + EPSILON)[:, None, None] * pair_gain[1][None]
    ).astype(jnp.bfloat16)
    stacked = jnp.stack([queries, keys_part, values_part])
    mine = lax.dynamic_index_in_dim(stacked, core, axis=2, keepdims=False)
    theirs = lax.dynamic_index_in_dim(stacked, 1 - core, axis=2, keepdims=False)
    got = lax.ppermute(theirs, "core", swap)
    first_half = jnp.where(core == 0, mine, got).reshape(3, chips, piece, HEAD_DIM)
    second_half = jnp.where(core == 0, got, mine).reshape(3, chips, piece, HEAD_DIM)
    whole = jnp.stack([first_half, second_half], axis=2).reshape(3, groups * piece, HEAD_DIM)
    length = whole.shape[1]
    factor = HEAD_DIM ** (-0.5)
    covered = SLOTS * TILE
    tile_query = whole[0, :covered].reshape(SLOTS, TILE, HEAD_DIM)
    tile_key = whole[1, :covered].reshape(SLOTS, TILE, HEAD_DIM)
    tile_value = whole[2, :covered].reshape(SLOTS, TILE, HEAD_DIM)
    scores = (
        jnp.einsum("sqc,skc->sqk", tile_query, tile_key, preferred_element_type=jnp.float32)
        * factor
    )
    highest = jnp.max(scores, axis=-1, keepdims=True)
    exponent = jnp.exp(scores - highest)
    weights = (exponent / jnp.sum(exponent, axis=-1, keepdims=True)).astype(jnp.bfloat16)
    tile_out = jnp.einsum(
        "sqk,skc->sqc", weights, tile_value, preferred_element_type=jnp.float32
    ).astype(jnp.bfloat16)
    head_out = jnp.concatenate(
        [
            tile_out.reshape(covered, HEAD_DIM),
            jnp.zeros((length - covered, HEAD_DIM), jnp.bfloat16),
        ],
        axis=0,
    )
    holder, living = tile_owners(tile_counts, owners)
    own_holder = holder[row_index]
    own_living = living[row_index]
    destination = jnp.arange(row_count, dtype=jnp.int32)[:, None]
    sending = jnp.logical_and(destination == own_holder[None, :], own_living[None, :])
    by_block = head_out.reshape(chips, cores, piece, HEAD_DIM)
    pair_heads = pair_weight.reshape(groups, HEAD_DIM, cores * block)
    pair_tokens = lax.dynamic_slice_in_dim(half, chip * cores * block, cores * block, axis=1)
    pair_scale = lax.dynamic_slice_in_dim(layer_scale, chip * cores * block, cores * block)
    parts = 2
    span = chips // parts
    part_rows = span * piece
    finished = []
    slot_received = []
    for part in range(parts):
        chosen = by_block[part * span : (part + 1) * span].transpose(1, 0, 2, 3)
        chosen = chosen.reshape(cores, part_rows, HEAD_DIM)
        outgoing = jnp.broadcast_to(chosen[None], (chips, cores, part_rows, HEAD_DIM))
        all_heads = lax.all_to_all(
            outgoing.reshape(groups, part_rows, HEAD_DIM),
            ("chip", "core"),
            split_axis=0,
            concat_axis=0,
            tiled=True,
        )
        if slot_received:
            all_heads, slot_received[-1] = lax.optimization_barrier((all_heads, slot_received[-1]))
        head_terms = jnp.einsum(
            "hsc,hcd->hsd", all_heads, pair_heads, preferred_element_type=jnp.float32
        ).astype(jnp.bfloat16)
        attention = jnp.sum(lax.optimization_barrier(head_terms).astype(jnp.float32), axis=0)
        rows = pair_tokens[part * part_rows : (part + 1) * part_rows]
        updated_half = (rows.astype(jnp.float32) + pair_scale * attention).astype(jnp.bfloat16)
        keep = lax.dynamic_slice_in_dim(updated_half, core * block, block, axis=1)
        give = lax.dynamic_slice_in_dim(updated_half, (1 - core) * block, block, axis=1)
        taken = lax.ppermute(give, "core", swap)
        first_half = jnp.where(core == 0, keep, taken).reshape(span, piece, block)
        second_half = jnp.where(core == 0, taken, keep).reshape(span, piece, block)
        finished.append(
            jnp.stack([first_half, second_half], axis=1).reshape(span * cores * piece, block)
        )
        done = jnp.concatenate(finished, axis=0) if len(finished) > 1 else finished[0]
        tile_slot = part
        first = tile_slot * TILE
        merged = merge_one(done[first + 1 : first + TILE])
        outgoing = jnp.where(
            sending[:, tile_slot, None, None], merged[None], jnp.zeros((), jnp.bfloat16)
        )
        slot_received.append(
            lax.all_to_all(outgoing, "fsdp", split_axis=0, concat_axis=0, tiled=True)
        )
    received = jnp.stack(slot_received, axis=1)
    return place_tiles(received, holder, living, row_index)


def solution(mesh):
    fsdp_size = mesh.shape["fsdp"]
    dp_size = mesh.shape["dp"]
    split = Mesh(
        mesh.devices.reshape(fsdp_size, dp_size // 2, 2), ("fsdp", "chip", "core")
    )
    heads = ("chip", "core")
    placed = (
        P("fsdp", heads, None),
        P(),
        P("fsdp", heads),
        P(None, heads),
        P(heads, "fsdp"),
        P(),
        P(),
        P(),
    )
    return jax.shard_map(
        body, mesh=split, in_specs=placed, out_specs=P("fsdp", None, heads), check_vma=False
    )
```

```python
import jax
import jax.numpy as jnp
from jax import lax
from jax.sharding import PartitionSpec as P

HEAD_DIM = 128
GRID = 32
SLOTS = 2
TILE = 1025
CAP = 4


EPSILON = 1e-06


def merge_tiles(values):
    halves = GRID // 2
    columns = values.shape[1]
    tile_list = []
    for tile_slot in range(SLOTS):
        patches = values[tile_slot * TILE + 1 : (tile_slot + 1) * TILE]
        square = patches.reshape(halves, 2, halves, 2, columns).transpose(0, 2, 4, 1, 3)
        tile_list.append(square.reshape(halves * halves, columns * 4))
    return jnp.stack(tile_list)


def tile_owners(tile_counts, owners):
    slot_index = jnp.arange(SLOTS, dtype=jnp.int32)[None, :]
    first_count = tile_counts[:, 0:1]
    holder = jnp.where(slot_index < first_count, owners[:, 0:1], owners[:, 1:2])
    living = slot_index < first_count + tile_counts[:, 1:2]
    return (holder, living)


def place_tiles(received, holder, living, target):
    owned_flag = jnp.logical_and(living, holder == target).reshape(-1).astype(jnp.int32)
    before = jnp.cumsum(owned_flag) - owned_flag
    flattened = received.reshape((received.shape[0] * received.shape[1],) + received.shape[2:])
    sources = jnp.arange(flattened.shape[0], dtype=jnp.int32)
    placed = []
    for slot in range(CAP):
        match = jnp.logical_and(before == slot, owned_flag == 1)
        source = jnp.max(jnp.where(match, sources, 0))
        tile = lax.dynamic_index_in_dim(flattened, source, axis=0, keepdims=False)
        placed.append(jnp.where(jnp.any(match), tile, jnp.zeros((), tile.dtype)))
    return jnp.stack(placed)


def gather_sum(values, axis_name, groups):
    spread = jnp.broadcast_to(values[None], (groups,) + values.shape)
    collected = lax.all_to_all(spread, axis_name, split_axis=0, concat_axis=0, tiled=True)
    return jnp.sum(collected, axis=0)


def gather_blocks(block_value, axis_name, groups):
    spread = jnp.broadcast_to(block_value[None], (groups,) + block_value.shape)
    collected = lax.all_to_all(spread, axis_name, split_axis=0, concat_axis=0, tiled=True)
    return collected.reshape((groups * block_value.shape[0],) + block_value.shape[1:])


def body(tokens, norm_gain, qkv_weight, qk_gain, out_weight, layer_scale, tile_counts, owners):
    own_rows = tokens[0]
    groups = lax.axis_size("dp")
    dp_index = lax.axis_index("dp")
    row_index = lax.axis_index("fsdp")
    row_count = lax.axis_size("fsdp")
    model_width = own_rows.shape[1]
    block = model_width // groups
    full_qkv = gather_blocks(qkv_weight, "fsdp", row_count)
    gathered = lax.all_gather(own_rows, "dp", axis=0, tiled=True)
    values = gathered.astype(jnp.float32)
    normed = (
        values * lax.rsqrt(jnp.mean(values * values, axis=-1, keepdims=True) + EPSILON) * norm_gain
    ).astype(jnp.bfloat16)
    projected = jnp.dot(normed, full_qkv, preferred_element_type=jnp.float32)
    queries = projected[:, :HEAD_DIM]
    keys_part = projected[:, HEAD_DIM : 2 * HEAD_DIM]
    values_part = projected[:, 2 * HEAD_DIM :].astype(jnp.bfloat16)
    sums = gather_sum(
        jnp.stack([jnp.sum(queries * queries, axis=-1), jnp.sum(keys_part * keys_part, axis=-1)]),
        "dp",
        groups,
    )
    window = groups * HEAD_DIM
    queries = (queries * lax.rsqrt(sums[0] / window + EPSILON)[:, None] * qk_gain[0]).astype(
        jnp.bfloat16
    )
    keys_part = (keys_part * lax.rsqrt(sums[1] / window + EPSILON)[:, None] * qk_gain[1]).astype(
        jnp.bfloat16
    )
    factor = HEAD_DIM ** (-0.5)
    own_block = lax.dynamic_slice_in_dim(gathered, dp_index * block, block, axis=1)
    scale_block = lax.dynamic_slice_in_dim(layer_scale, dp_index * block, block)
    holder, living = tile_owners(tile_counts, owners)
    own_holder = holder[row_index]
    own_living = living[row_index]
    destination = jnp.arange(row_count, dtype=jnp.int32)[:, None]
    sending = jnp.logical_and(destination == own_holder[None, :], own_living[None, :])
    halves = GRID // 2
    slot_received = []
    for tile_slot in range(SLOTS):
        first = tile_slot * TILE
        tile_query = queries[first : first + TILE]
        tile_key = keys_part[first : first + TILE]
        tile_value = values_part[first : first + TILE]
        scores = jnp.dot(tile_query[1:], tile_key.T, preferred_element_type=jnp.float32) * factor
        highest = jnp.max(scores, axis=-1, keepdims=True)
        exponent = jnp.exp(scores - highest)
        weights = (exponent / jnp.sum(exponent, axis=-1, keepdims=True)).astype(jnp.bfloat16)
        tile_out = jnp.dot(weights, tile_value, preferred_element_type=jnp.float32).astype(
            jnp.bfloat16
        )
        if not slot_received:
            late_weight, tile_out = lax.optimization_barrier((out_weight, tile_out))
        all_heads = lax.all_gather(tile_out, "dp", axis=0, tiled=False)
        if not slot_received:
            head_rows = lax.all_gather(late_weight, "fsdp", axis=1, tiled=True)
            weight_block = lax.all_to_all(
                head_rows, "dp", split_axis=1, concat_axis=0, tiled=True
            )
        if slot_received:
            all_heads, slot_received[-1] = lax.optimization_barrier((all_heads, slot_received[-1]))
        head_terms = jnp.einsum(
            "hsc,hcd->hsd",
            all_heads,
            weight_block.reshape(groups, HEAD_DIM, block),
            preferred_element_type=jnp.float32,
        ).astype(jnp.bfloat16)
        attention = jnp.sum(lax.optimization_barrier(head_terms).astype(jnp.float32), axis=0)
        patches = own_block[first + 1 : first + TILE]
        updated = (patches.astype(jnp.float32) + scale_block * attention).astype(jnp.bfloat16)
        square = updated.reshape(halves, 2, halves, 2, block).transpose(0, 2, 4, 1, 3)
        merged = square.reshape(halves * halves, block * 4)
        outgoing = jnp.where(
            sending[:, tile_slot, None, None], merged[None], jnp.zeros((), jnp.bfloat16)
        )
        slot_received.append(
            lax.all_to_all(outgoing, "fsdp", split_axis=0, concat_axis=0, tiled=True)
        )
    received = jnp.stack(slot_received, axis=1)
    return place_tiles(received, holder, living, row_index)


def solution(mesh):
    placed = (
        P("fsdp", "dp", None),
        P(),
        P("fsdp", "dp"),
        P(None, "dp"),
        P("dp", "fsdp"),
        P(),
        P(),
        P(),
    )
    return jax.shard_map(
        body, mesh=mesh, in_specs=placed, out_specs=P("fsdp", None, "dp"), check_vma=False
    )
```

```python
import jax
import jax.numpy as jnp
from jax import lax
from jax.sharding import PartitionSpec as P

HEAD_DIM = 128
GRID = 32
SLOTS = 2
TILE = 1025
CAP = 4


EPSILON = 1e-06


def merge_tiles(values):
    halves = GRID // 2
    columns = values.shape[1]
    tile_list = []
    for tile_slot in range(SLOTS):
        patches = values[tile_slot * TILE + 1 : (tile_slot + 1) * TILE]
        square = patches.reshape(halves, 2, halves, 2, columns).transpose(0, 2, 4, 1, 3)
        tile_list.append(square.reshape(halves * halves, columns * 4))
    return jnp.stack(tile_list)


def tile_owners(tile_counts, owners):
    slot_index = jnp.arange(SLOTS, dtype=jnp.int32)[None, :]
    first_count = tile_counts[:, 0:1]
    holder = jnp.where(slot_index < first_count, owners[:, 0:1], owners[:, 1:2])
    living = slot_index < first_count + tile_counts[:, 1:2]
    return (holder, living)


def place_tiles(received, holder, living, target):
    owned_flag = jnp.logical_and(living, holder == target).reshape(-1).astype(jnp.int32)
    before = jnp.cumsum(owned_flag) - owned_flag
    flattened = received.reshape((received.shape[0] * received.shape[1],) + received.shape[2:])
    sources = jnp.arange(flattened.shape[0], dtype=jnp.int32)
    placed = []
    for slot in range(CAP):
        match = jnp.logical_and(before == slot, owned_flag == 1)
        source = jnp.max(jnp.where(match, sources, 0))
        tile = lax.dynamic_index_in_dim(flattened, source, axis=0, keepdims=False)
        placed.append(jnp.where(jnp.any(match), tile, jnp.zeros((), tile.dtype)))
    return jnp.stack(placed)


def gather_sum(values, axis_name, groups):
    spread = jnp.broadcast_to(values[None], (groups,) + values.shape)
    collected = lax.all_to_all(spread, axis_name, split_axis=0, concat_axis=0, tiled=True)
    return jnp.sum(collected, axis=0)


def gather_blocks(block_value, axis_name, groups):
    spread = jnp.broadcast_to(block_value[None], (groups,) + block_value.shape)
    collected = lax.all_to_all(spread, axis_name, split_axis=0, concat_axis=0, tiled=True)
    return collected.reshape((groups * block_value.shape[0],) + block_value.shape[1:])


def body(tokens, norm_gain, qkv_weight, qk_gain, out_weight, layer_scale, tile_counts, owners):
    own_rows = tokens[0]
    groups = lax.axis_size("dp")
    dp_index = lax.axis_index("dp")
    row_index = lax.axis_index("fsdp")
    row_count = lax.axis_size("fsdp")
    model_width = own_rows.shape[1]
    block = model_width // groups
    full_qkv = gather_blocks(qkv_weight, "fsdp", row_count)
    gathered = lax.all_gather(own_rows, "dp", axis=0, tiled=True)
    values = gathered.astype(jnp.float32)
    normed = (
        values * lax.rsqrt(jnp.mean(values * values, axis=-1, keepdims=True) + EPSILON) * norm_gain
    ).astype(jnp.bfloat16)
    projected = jnp.dot(normed, full_qkv, preferred_element_type=jnp.float32)
    queries = projected[:, :HEAD_DIM]
    keys_part = projected[:, HEAD_DIM : 2 * HEAD_DIM]
    values_part = projected[:, 2 * HEAD_DIM :].astype(jnp.bfloat16)
    sums = gather_sum(
        jnp.stack([jnp.sum(queries * queries, axis=-1), jnp.sum(keys_part * keys_part, axis=-1)]),
        "dp",
        groups,
    )
    window = groups * HEAD_DIM
    queries = (queries * lax.rsqrt(sums[0] / window + EPSILON)[:, None] * qk_gain[0]).astype(
        jnp.bfloat16
    )
    keys_part = (keys_part * lax.rsqrt(sums[1] / window + EPSILON)[:, None] * qk_gain[1]).astype(
        jnp.bfloat16
    )
    factor = HEAD_DIM ** (-0.5)
    own_block = lax.dynamic_slice_in_dim(gathered, dp_index * block, block, axis=1)
    scale_block = lax.dynamic_slice_in_dim(layer_scale, dp_index * block, block)
    holder, living = tile_owners(tile_counts, owners)
    own_holder = holder[row_index]
    own_living = living[row_index]
    destination = jnp.arange(row_count, dtype=jnp.int32)[:, None]
    sending = jnp.logical_and(destination == own_holder[None, :], own_living[None, :])
    halves = GRID // 2
    slot_received = []
    for tile_slot in range(SLOTS):
        first = tile_slot * TILE
        tile_query = queries[first : first + TILE]
        tile_key = keys_part[first : first + TILE]
        tile_value = values_part[first : first + TILE]
        scores = jnp.dot(tile_query[1:], tile_key.T, preferred_element_type=jnp.float32) * factor
        highest = jnp.max(scores, axis=-1, keepdims=True)
        exponent = jnp.exp(scores - highest)
        weights = (exponent / jnp.sum(exponent, axis=-1, keepdims=True)).astype(jnp.bfloat16)
        tile_out = jnp.dot(weights, tile_value, preferred_element_type=jnp.float32).astype(
            jnp.bfloat16
        )
        if not slot_received:
            late_weight, tile_out = lax.optimization_barrier((out_weight, tile_out))
        pieces = 2
        piece_rows = tile_out.shape[0] // pieces
        piece_received = []
        for piece in range(pieces):
            piece_out = tile_out[piece * piece_rows : (piece + 1) * piece_rows]
            all_heads = lax.all_gather(piece_out, "dp", axis=0, tiled=False)
            if not slot_received and not piece_received:
                head_rows = lax.all_gather(late_weight, "fsdp", axis=1, tiled=True)
                weight_block = lax.all_to_all(
                    head_rows, "dp", split_axis=1, concat_axis=0, tiled=True
                )
            last = piece_received if piece_received else slot_received
            if last:
                all_heads, last[-1] = lax.optimization_barrier((all_heads, last[-1]))
            head_terms = jnp.einsum(
                "hsc,hcd->hsd",
                all_heads,
                weight_block.reshape(groups, HEAD_DIM, block),
                preferred_element_type=jnp.float32,
            ).astype(jnp.bfloat16)
            attention = jnp.sum(lax.optimization_barrier(head_terms).astype(jnp.float32), axis=0)
            start = first + 1 + piece * piece_rows
            patches = own_block[start : start + piece_rows]
            updated = (patches.astype(jnp.float32) + scale_block * attention).astype(jnp.bfloat16)
            square = updated.reshape(halves // pieces, 2, halves, 2, block).transpose(0, 2, 4, 1, 3)
            merged = square.reshape(halves * halves // pieces, block * 4)
            outgoing = jnp.where(
                sending[:, tile_slot, None, None], merged[None], jnp.zeros((), jnp.bfloat16)
            )
            piece_received.append(
                lax.all_to_all(outgoing, "fsdp", split_axis=0, concat_axis=0, tiled=True)
            )
        slot_received.append(jnp.concatenate(piece_received, axis=1))
    received = jnp.stack(slot_received, axis=1)
    return place_tiles(received, holder, living, row_index)


def solution(mesh):
    placed = (
        P("fsdp", "dp", None),
        P(),
        P("fsdp", "dp"),
        P(None, "dp"),
        P("dp", "fsdp"),
        P(),
        P(),
        P(),
    )
    return jax.shard_map(
        body, mesh=mesh, in_specs=placed, out_specs=P("fsdp", None, "dp"), check_vma=False
    )
```

```python
import jax
import jax.numpy as jnp
from jax import lax
from jax.sharding import PartitionSpec as P

HEAD_DIM = 128
GRID = 32
SLOTS = 2
TILE = 1025
CAP = 4


EPSILON = 1e-06


def merge_tiles(values):
    halves = GRID // 2
    columns = values.shape[1]
    tile_list = []
    for tile_slot in range(SLOTS):
        patches = values[tile_slot * TILE + 1 : (tile_slot + 1) * TILE]
        square = patches.reshape(halves, 2, halves, 2, columns).transpose(0, 2, 4, 1, 3)
        tile_list.append(square.reshape(halves * halves, columns * 4))
    return jnp.stack(tile_list)


def tile_owners(tile_counts, owners):
    slot_index = jnp.arange(SLOTS, dtype=jnp.int32)[None, :]
    first_count = tile_counts[:, 0:1]
    holder = jnp.where(slot_index < first_count, owners[:, 0:1], owners[:, 1:2])
    living = slot_index < first_count + tile_counts[:, 1:2]
    return (holder, living)


def place_tiles(received, holder, living, target):
    owned_flag = jnp.logical_and(living, holder == target).reshape(-1).astype(jnp.int32)
    before = jnp.cumsum(owned_flag) - owned_flag
    flattened = received.reshape((received.shape[0] * received.shape[1],) + received.shape[2:])
    sources = jnp.arange(flattened.shape[0], dtype=jnp.int32)
    placed = []
    for slot in range(CAP):
        match = jnp.logical_and(before == slot, owned_flag == 1)
        source = jnp.max(jnp.where(match, sources, 0))
        tile = lax.dynamic_index_in_dim(flattened, source, axis=0, keepdims=False)
        placed.append(jnp.where(jnp.any(match), tile, jnp.zeros((), tile.dtype)))
    return jnp.stack(placed)


def gather_sum(values, axis_name, groups):
    spread = jnp.broadcast_to(values[None], (groups,) + values.shape)
    collected = lax.all_to_all(spread, axis_name, split_axis=0, concat_axis=0, tiled=True)
    return jnp.sum(collected, axis=0)


def gather_blocks(block_value, axis_name, groups):
    spread = jnp.broadcast_to(block_value[None], (groups,) + block_value.shape)
    collected = lax.all_to_all(spread, axis_name, split_axis=0, concat_axis=0, tiled=True)
    return collected.reshape((groups * block_value.shape[0],) + block_value.shape[1:])


def body(tokens, norm_gain, qkv_weight, qk_gain, out_weight, layer_scale, tile_counts, owners):
    own_rows = tokens[0]
    groups = lax.axis_size("dp")
    dp_index = lax.axis_index("dp")
    row_index = lax.axis_index("fsdp")
    row_count = lax.axis_size("fsdp")
    model_width = own_rows.shape[1]
    block = model_width // groups
    full_qkv = gather_blocks(qkv_weight, "fsdp", row_count)
    gathered = lax.all_gather(own_rows, "dp", axis=0, tiled=True)
    values = gathered.astype(jnp.float32)
    normed = (
        values * lax.rsqrt(jnp.mean(values * values, axis=-1, keepdims=True) + EPSILON) * norm_gain
    ).astype(jnp.bfloat16)
    projected = jnp.dot(normed, full_qkv, preferred_element_type=jnp.float32)
    queries = projected[:, :HEAD_DIM]
    keys_part = projected[:, HEAD_DIM : 2 * HEAD_DIM]
    values_part = projected[:, 2 * HEAD_DIM :].astype(jnp.bfloat16)
    sums = gather_sum(
        jnp.stack([jnp.sum(queries * queries, axis=-1), jnp.sum(keys_part * keys_part, axis=-1)]),
        "dp",
        groups,
    )
    window = groups * HEAD_DIM
    queries = (queries * lax.rsqrt(sums[0] / window + EPSILON)[:, None] * qk_gain[0]).astype(
        jnp.bfloat16
    )
    keys_part = (keys_part * lax.rsqrt(sums[1] / window + EPSILON)[:, None] * qk_gain[1]).astype(
        jnp.bfloat16
    )
    factor = HEAD_DIM ** (-0.5)
    own_block = lax.dynamic_slice_in_dim(gathered, dp_index * block, block, axis=1)
    scale_block = lax.dynamic_slice_in_dim(layer_scale, dp_index * block, block)
    holder, living = tile_owners(tile_counts, owners)
    own_holder = holder[row_index]
    own_living = living[row_index]
    destination = jnp.arange(row_count, dtype=jnp.int32)[:, None]
    sending = jnp.logical_and(destination == own_holder[None, :], own_living[None, :])
    outs = []
    for tile_slot in range(SLOTS):
        first = tile_slot * TILE
        tile_query = queries[first : first + TILE]
        tile_key = keys_part[first : first + TILE]
        tile_value = values_part[first : first + TILE]
        scores = jnp.dot(tile_query[1:], tile_key.T, preferred_element_type=jnp.float32) * factor
        highest = jnp.max(scores, axis=-1, keepdims=True)
        exponent = jnp.exp(scores - highest)
        weights = (exponent / jnp.sum(exponent, axis=-1, keepdims=True)).astype(jnp.bfloat16)
        outs.append(
            jnp.dot(weights, tile_value, preferred_element_type=jnp.float32).astype(jnp.bfloat16)
        )
    tile_out = jnp.stack(outs)
    late_weight, tile_out = lax.optimization_barrier((out_weight, tile_out))
    all_heads = lax.all_gather(tile_out, "dp", axis=0, tiled=False)
    head_rows = lax.all_gather(late_weight, "fsdp", axis=1, tiled=True)
    weight_block = lax.all_to_all(head_rows, "dp", split_axis=1, concat_axis=0, tiled=True)
    head_terms = jnp.einsum(
        "htsc,hcd->htsd",
        all_heads,
        weight_block.reshape(groups, HEAD_DIM, block),
        preferred_element_type=jnp.float32,
    ).astype(jnp.bfloat16)
    attention = jnp.sum(lax.optimization_barrier(head_terms).astype(jnp.float32), axis=0)
    patches = jnp.stack(
        [own_block[slot * TILE + 1 : (slot + 1) * TILE] for slot in range(SLOTS)]
    )
    updated = (patches.astype(jnp.float32) + scale_block * attention).astype(jnp.bfloat16)
    halves = GRID // 2
    square = updated.reshape(SLOTS, halves, 2, halves, 2, block).transpose(0, 1, 3, 5, 2, 4)
    merged = square.reshape(SLOTS, halves * halves, block * 4)
    outgoing = jnp.where(sending[:, :, None, None], merged[None], jnp.zeros((), jnp.bfloat16))
    received = lax.all_to_all(outgoing, "fsdp", split_axis=0, concat_axis=0, tiled=True)
    return place_tiles(received, holder, living, row_index)


def solution(mesh):
    placed = (
        P("fsdp", "dp", None),
        P(),
        P("fsdp", "dp"),
        P(None, "dp"),
        P("dp", "fsdp"),
        P(),
        P(),
        P(),
    )
    return jax.shard_map(
        body, mesh=mesh, in_specs=placed, out_specs=P("fsdp", None, "dp"), check_vma=False
    )
```

```python
import jax
import jax.numpy as jnp
from jax import lax
from jax.sharding import PartitionSpec as P

HEAD_DIM = 128
GRID = 32
SLOTS = 2
TILE = 1025
CAP = 4


EPSILON = 1e-06


def merge_tiles(values):
    halves = GRID // 2
    columns = values.shape[1]
    tile_list = []
    for tile_slot in range(SLOTS):
        patches = values[tile_slot * TILE + 1 : (tile_slot + 1) * TILE]
        square = patches.reshape(halves, 2, halves, 2, columns).transpose(0, 2, 4, 1, 3)
        tile_list.append(square.reshape(halves * halves, columns * 4))
    return jnp.stack(tile_list)


def tile_owners(tile_counts, owners):
    slot_index = jnp.arange(SLOTS, dtype=jnp.int32)[None, :]
    first_count = tile_counts[:, 0:1]
    holder = jnp.where(slot_index < first_count, owners[:, 0:1], owners[:, 1:2])
    living = slot_index < first_count + tile_counts[:, 1:2]
    return (holder, living)


def place_tiles(received, holder, living, target, shifted_from=None):
    owned_flag = jnp.logical_and(living, holder == target).reshape(-1).astype(jnp.int32)
    before = jnp.cumsum(owned_flag) - owned_flag
    flattened = received.reshape((received.shape[0] * received.shape[1],) + received.shape[2:])
    sources = jnp.arange(flattened.shape[0], dtype=jnp.int32)
    if shifted_from is not None:
        rows = received.shape[0]
        slots = received.shape[1]
        sources = ((shifted_from - sources // slots) % rows) * slots + sources % slots
    placed = []
    for slot in range(CAP):
        match = jnp.logical_and(before == slot, owned_flag == 1)
        source = jnp.max(jnp.where(match, sources, 0))
        tile = lax.dynamic_index_in_dim(flattened, source, axis=0, keepdims=False)
        placed.append(jnp.where(jnp.any(match), tile, jnp.zeros((), tile.dtype)))
    return jnp.stack(placed)


def gather_sum(values, axis_name, groups):
    spread = jnp.broadcast_to(values[None], (groups,) + values.shape)
    collected = lax.all_to_all(spread, axis_name, split_axis=0, concat_axis=0, tiled=True)
    return jnp.sum(collected, axis=0)


def gather_blocks(block_value, axis_name, groups):
    spread = jnp.broadcast_to(block_value[None], (groups,) + block_value.shape)
    collected = lax.all_to_all(spread, axis_name, split_axis=0, concat_axis=0, tiled=True)
    return collected.reshape((groups * block_value.shape[0],) + block_value.shape[1:])


def body(tokens, norm_gain, qkv_weight, qk_gain, out_weight, layer_scale, tile_counts, owners):
    own_rows = tokens[0]
    groups = lax.axis_size("dp")
    dp_index = lax.axis_index("dp")
    row_index = lax.axis_index("fsdp")
    row_count = lax.axis_size("fsdp")
    model_width = own_rows.shape[1]
    block = model_width // groups
    full_qkv = gather_blocks(qkv_weight, "fsdp", row_count)
    gathered = lax.all_gather(own_rows, "dp", axis=0, tiled=True)
    values = gathered.astype(jnp.float32)
    normed = (
        values * lax.rsqrt(jnp.mean(values * values, axis=-1, keepdims=True) + EPSILON) * norm_gain
    ).astype(jnp.bfloat16)
    projected = jnp.dot(normed, full_qkv, preferred_element_type=jnp.float32)
    queries = projected[:, :HEAD_DIM]
    keys_part = projected[:, HEAD_DIM : 2 * HEAD_DIM]
    values_part = projected[:, 2 * HEAD_DIM :].astype(jnp.bfloat16)
    sums = gather_sum(
        jnp.stack([jnp.sum(queries * queries, axis=-1), jnp.sum(keys_part * keys_part, axis=-1)]),
        "dp",
        groups,
    )
    window = groups * HEAD_DIM
    queries = (queries * lax.rsqrt(sums[0] / window + EPSILON)[:, None] * qk_gain[0]).astype(
        jnp.bfloat16
    )
    keys_part = (keys_part * lax.rsqrt(sums[1] / window + EPSILON)[:, None] * qk_gain[1]).astype(
        jnp.bfloat16
    )
    factor = HEAD_DIM ** (-0.5)
    own_block = lax.dynamic_slice_in_dim(gathered, dp_index * block, block, axis=1)
    scale_block = lax.dynamic_slice_in_dim(layer_scale, dp_index * block, block)
    holder, living = tile_owners(tile_counts, owners)
    own_holder = holder[row_index]
    own_living = living[row_index]
    destination = jnp.arange(row_count, dtype=jnp.int32)[:, None]
    sending = jnp.logical_and(destination == own_holder[None, :], own_living[None, :])
    outs = []
    for tile_slot in range(SLOTS):
        first = tile_slot * TILE
        tile_query = queries[first : first + TILE]
        tile_key = keys_part[first : first + TILE]
        tile_value = values_part[first : first + TILE]
        scores = jnp.dot(tile_query[1:], tile_key.T, preferred_element_type=jnp.float32) * factor
        highest = jnp.max(scores, axis=-1, keepdims=True)
        exponent = jnp.exp(scores - highest)
        weights = (exponent / jnp.sum(exponent, axis=-1, keepdims=True)).astype(jnp.bfloat16)
        outs.append(
            jnp.dot(weights, tile_value, preferred_element_type=jnp.float32).astype(jnp.bfloat16)
        )
    tile_out = jnp.stack(outs)
    late_weight, tile_out = lax.optimization_barrier((out_weight, tile_out))
    all_heads = lax.all_gather(tile_out, "dp", axis=0, tiled=False)
    head_rows = lax.all_gather(late_weight, "fsdp", axis=1, tiled=True)
    weight_block = lax.all_to_all(head_rows, "dp", split_axis=1, concat_axis=0, tiled=True)
    head_terms = jnp.einsum(
        "htsc,hcd->htsd",
        all_heads,
        weight_block.reshape(groups, HEAD_DIM, block),
        preferred_element_type=jnp.float32,
    ).astype(jnp.bfloat16)
    attention = jnp.sum(lax.optimization_barrier(head_terms).astype(jnp.float32), axis=0)
    patches = jnp.stack(
        [own_block[slot * TILE + 1 : (slot + 1) * TILE] for slot in range(SLOTS)]
    )
    updated = (patches.astype(jnp.float32) + scale_block * attention).astype(jnp.bfloat16)
    halves = GRID // 2
    square = updated.reshape(SLOTS, halves, 2, halves, 2, block).transpose(0, 1, 3, 5, 2, 4)
    merged = square.reshape(SLOTS, halves * halves, block * 4)
    zero = jnp.zeros((), jnp.bfloat16)
    arrived = [None] * row_count
    arrived[0] = jnp.where(sending[row_index][:, None, None], merged, zero)
    for shift in range(1, row_count):
        target = (row_index + shift) % row_count
        outgoing = jnp.where(sending[target][:, None, None], merged, zero)
        ring = [(source, (source + shift) % row_count) for source in range(row_count)]
        arrived[shift] = lax.ppermute(outgoing, "fsdp", ring)
    by_shift = jnp.stack(arrived)
    return place_tiles(by_shift, holder, living, row_index, row_index)


def solution(mesh):
    placed = (
        P("fsdp", "dp", None),
        P(),
        P("fsdp", "dp"),
        P(None, "dp"),
        P("dp", "fsdp"),
        P(),
        P(),
        P(),
    )
    return jax.shard_map(
        body, mesh=mesh, in_specs=placed, out_specs=P("fsdp", None, "dp"), check_vma=False
    )
```

```python
import jax
import jax.numpy as jnp
from jax import lax
from jax.sharding import Mesh, PartitionSpec as P

HEAD_DIM = 128
GRID = 32
SLOTS = 2
TILE = 1025
CAP = 4


EPSILON = 1e-06


def merge_tiles(values):
    halves = GRID // 2
    columns = values.shape[1]
    tile_list = []
    for tile_slot in range(SLOTS):
        patches = values[tile_slot * TILE + 1 : (tile_slot + 1) * TILE]
        square = patches.reshape(halves, 2, halves, 2, columns).transpose(0, 2, 4, 1, 3)
        tile_list.append(square.reshape(halves * halves, columns * 4))
    return jnp.stack(tile_list)


def tile_owners(tile_counts, owners):
    slot_index = jnp.arange(SLOTS, dtype=jnp.int32)[None, :]
    first_count = tile_counts[:, 0:1]
    holder = jnp.where(slot_index < first_count, owners[:, 0:1], owners[:, 1:2])
    living = slot_index < first_count + tile_counts[:, 1:2]
    return (holder, living)


def place_tiles(received, holder, living, target):
    owned_flag = jnp.logical_and(living, holder == target).reshape(-1).astype(jnp.int32)
    before = jnp.cumsum(owned_flag) - owned_flag
    flattened = received.reshape((received.shape[0] * received.shape[1],) + received.shape[2:])
    sources = jnp.arange(flattened.shape[0], dtype=jnp.int32)
    placed = []
    for slot in range(CAP):
        match = jnp.logical_and(before == slot, owned_flag == 1)
        source = jnp.max(jnp.where(match, sources, 0))
        tile = lax.dynamic_index_in_dim(flattened, source, axis=0, keepdims=False)
        placed.append(jnp.where(jnp.any(match), tile, jnp.zeros((), tile.dtype)))
    return jnp.stack(placed)


def gather_sum(values, axis_name, groups):
    spread = jnp.broadcast_to(values[None], (groups,) + values.shape)
    collected = lax.all_to_all(spread, axis_name, split_axis=0, concat_axis=0, tiled=True)
    return jnp.sum(collected, axis=0)


def gather_blocks(block_value, axis_name, groups):
    spread = jnp.broadcast_to(block_value[None], (groups,) + block_value.shape)
    collected = lax.all_to_all(spread, axis_name, split_axis=0, concat_axis=0, tiled=True)
    return collected.reshape((groups * block_value.shape[0],) + block_value.shape[1:])


def pair_up(value, core, swap, axis):
    other = lax.ppermute(value, "core", swap)
    low = jnp.where(core == 0, value, other)
    high = jnp.where(core == 0, other, value)
    return jnp.concatenate([low, high], axis=axis)


def body(tokens, norm_gain, qkv_weight, qk_gain, out_weight, layer_scale, tile_counts, owners):
    own_rows = tokens[0]
    chips = lax.axis_size("chip")
    cores = lax.axis_size("core")
    groups = chips * cores
    chip = lax.axis_index("chip")
    core = lax.axis_index("core")
    row_index = lax.axis_index("fsdp")
    row_count = lax.axis_size("fsdp")
    model_width = own_rows.shape[1]
    block = model_width // groups
    swap = [(0, 1), (1, 0)]
    spread = jnp.broadcast_to(out_weight[None], (row_count,) + out_weight.shape)
    head_rows = lax.all_to_all(spread, "fsdp", split_axis=0, concat_axis=0, tiled=True)
    per_row = out_weight.shape[1] // block
    head_rows = head_rows.reshape(row_count, HEAD_DIM, per_row, block).transpose(0, 2, 1, 3)
    weight_block = lax.all_to_all(
        head_rows.reshape(groups, HEAD_DIM, block),
        ("chip", "core"),
        split_axis=0,
        concat_axis=0,
        tiled=True,
    ).reshape(groups * HEAD_DIM, block)
    pair_weight = pair_up(weight_block, core, swap, 1)
    full_qkv = gather_blocks(qkv_weight, "fsdp", row_count)
    pair_qkv = pair_up(full_qkv, core, swap, 1)
    pair_qkv, pair_weight = lax.optimization_barrier((pair_qkv, pair_weight))
    pair_gain = pair_up(qk_gain, core, swap, 1).reshape(2, cores, HEAD_DIM)
    half = lax.all_gather(own_rows, "chip", axis=0, tiled=True)
    half_length = half.shape[0]
    piece = own_rows.shape[0]
    values = half.astype(jnp.float32)
    normed = (
        values * lax.rsqrt(jnp.mean(values * values, axis=-1, keepdims=True) + EPSILON) * norm_gain
    ).astype(jnp.bfloat16)
    projected = jnp.dot(normed, pair_qkv, preferred_element_type=jnp.float32)
    projected = projected.reshape(half_length, cores, 3, HEAD_DIM)
    queries = projected[:, :, 0]
    keys_part = projected[:, :, 1]
    values_part = projected[:, :, 2].astype(jnp.bfloat16)
    sums = gather_sum(
        jnp.stack(
            [jnp.sum(queries * queries, axis=(1, 2)), jnp.sum(keys_part * keys_part, axis=(1, 2))]
        ),
        "chip",
        chips,
    )
    window = groups * HEAD_DIM
    queries = (
        queries * lax.rsqrt(sums[0] / window + EPSILON)[:, None, None] * pair_gain[0][None]
    ).astype(jnp.bfloat16)
    keys_part = (
        keys_part * lax.rsqrt(sums[1] / window + EPSILON)[:, None, None] * pair_gain[1][None]
    ).astype(jnp.bfloat16)
    stacked = jnp.stack([queries, keys_part, values_part])
    mine = lax.dynamic_index_in_dim(stacked, core, axis=2, keepdims=False)
    theirs = lax.dynamic_index_in_dim(stacked, 1 - core, axis=2, keepdims=False)
    got = lax.ppermute(theirs, "core", swap)
    first_half = jnp.where(core == 0, mine, got).reshape(3, chips, piece, HEAD_DIM)
    second_half = jnp.where(core == 0, got, mine).reshape(3, chips, piece, HEAD_DIM)
    whole = jnp.stack([first_half, second_half], axis=2).reshape(3, groups * piece, HEAD_DIM)
    length = whole.shape[1]
    factor = HEAD_DIM ** (-0.5)
    covered = SLOTS * TILE
    tile_query = whole[0, :covered].reshape(SLOTS, TILE, HEAD_DIM)
    tile_key = whole[1, :covered].reshape(SLOTS, TILE, HEAD_DIM)
    tile_value = whole[2, :covered].reshape(SLOTS, TILE, HEAD_DIM)
    scores = (
        jnp.einsum("sqc,skc->sqk", tile_query, tile_key, preferred_element_type=jnp.float32)
        * factor
    )
    highest = jnp.max(scores, axis=-1, keepdims=True)
    exponent = jnp.exp(scores - highest)
    weights = (exponent / jnp.sum(exponent, axis=-1, keepdims=True)).astype(jnp.bfloat16)
    tile_out = jnp.einsum(
        "sqk,skc->sqc", weights, tile_value, preferred_element_type=jnp.float32
    ).astype(jnp.bfloat16)
    head_out = jnp.concatenate(
        [
            tile_out.reshape(covered, HEAD_DIM),
            jnp.zeros((length - covered, HEAD_DIM), jnp.bfloat16),
        ],
        axis=0,
    )
    by_half = head_out.reshape(chips, cores, piece, HEAD_DIM).transpose(1, 0, 2, 3)
    by_half = by_half.reshape(cores, half_length, HEAD_DIM)
    outgoing = jnp.broadcast_to(by_half[None], (chips, cores, half_length, HEAD_DIM))
    all_heads = lax.all_to_all(
        outgoing.reshape(groups, half_length, HEAD_DIM),
        ("chip", "core"),
        split_axis=0,
        concat_axis=0,
        tiled=True,
    )
    head_terms = jnp.einsum(
        "hsc,hcd->hsd",
        all_heads,
        pair_weight.reshape(groups, HEAD_DIM, cores * block),
        preferred_element_type=jnp.float32,
    ).astype(jnp.bfloat16)
    attention = jnp.sum(lax.optimization_barrier(head_terms).astype(jnp.float32), axis=0)
    pair_tokens = lax.dynamic_slice_in_dim(half, chip * cores * block, cores * block, axis=1)
    pair_scale = lax.dynamic_slice_in_dim(layer_scale, chip * cores * block, cores * block)
    updated_half = (pair_tokens.astype(jnp.float32) + pair_scale * attention).astype(jnp.bfloat16)
    keep = lax.dynamic_slice_in_dim(updated_half, core * block, block, axis=1)
    give = lax.dynamic_slice_in_dim(updated_half, (1 - core) * block, block, axis=1)
    taken = lax.ppermute(give, "core", swap)
    first_half = jnp.where(core == 0, keep, taken).reshape(chips, piece, block)
    second_half = jnp.where(core == 0, taken, keep).reshape(chips, piece, block)
    updated = jnp.stack([first_half, second_half], axis=1).reshape(length, block)
    merged = merge_tiles(updated)
    holder, living = tile_owners(tile_counts, owners)
    own_holder = holder[row_index]
    own_living = living[row_index]
    destination = jnp.arange(row_count, dtype=jnp.int32)[:, None]
    sending = jnp.logical_and(destination == own_holder[None, :], own_living[None, :])
    outgoing = jnp.where(sending[:, :, None, None], merged[None], jnp.zeros((), jnp.bfloat16))
    received = lax.all_to_all(outgoing, "fsdp", split_axis=0, concat_axis=0, tiled=True)
    return place_tiles(received, holder, living, row_index)


def solution(mesh):
    fsdp_size = mesh.shape["fsdp"]
    dp_size = mesh.shape["dp"]
    split = Mesh(
        mesh.devices.reshape(fsdp_size, dp_size // 2, 2), ("fsdp", "chip", "core")
    )
    heads = ("chip", "core")
    placed = (
        P("fsdp", heads, None),
        P(),
        P("fsdp", heads),
        P(None, heads),
        P(heads, "fsdp"),
        P(),
        P(),
        P(),
    )
    return jax.shard_map(
        body, mesh=split, in_specs=placed, out_specs=P("fsdp", None, heads), check_vma=False
    )
```

```python
import jax
import jax.numpy as jnp
from jax import lax
from jax.experimental import pallas as pl
from jax.sharding import Mesh, PartitionSpec as P

HEAD_DIM = 128
GRID = 32
SLOTS = 2
TILE = 1025
CAP = 4


EPSILON = 1e-06


def merge_tiles(values):
    halves = GRID // 2
    columns = values.shape[1]
    tile_list = []
    for tile_slot in range(SLOTS):
        patches = values[tile_slot * TILE + 1 : (tile_slot + 1) * TILE]
        square = patches.reshape(halves, 2, halves, 2, columns).transpose(0, 2, 4, 1, 3)
        tile_list.append(square.reshape(halves * halves, columns * 4))
    return jnp.stack(tile_list)


def tile_owners(tile_counts, owners):
    slot_index = jnp.arange(SLOTS, dtype=jnp.int32)[None, :]
    first_count = tile_counts[:, 0:1]
    holder = jnp.where(slot_index < first_count, owners[:, 0:1], owners[:, 1:2])
    living = slot_index < first_count + tile_counts[:, 1:2]
    return (holder, living)


def place_tiles(received, holder, living, target):
    owned_flag = jnp.logical_and(living, holder == target).reshape(-1).astype(jnp.int32)
    before = jnp.cumsum(owned_flag) - owned_flag
    flattened = received.reshape((received.shape[0] * received.shape[1],) + received.shape[2:])
    sources = jnp.arange(flattened.shape[0], dtype=jnp.int32)
    placed = []
    for slot in range(CAP):
        match = jnp.logical_and(before == slot, owned_flag == 1)
        source = jnp.max(jnp.where(match, sources, 0))
        tile = lax.dynamic_index_in_dim(flattened, source, axis=0, keepdims=False)
        placed.append(jnp.where(jnp.any(match), tile, jnp.zeros((), tile.dtype)))
    return jnp.stack(placed)


def gather_sum(values, axis_name, groups):
    spread = jnp.broadcast_to(values[None], (groups,) + values.shape)
    collected = lax.all_to_all(spread, axis_name, split_axis=0, concat_axis=0, tiled=True)
    return jnp.sum(collected, axis=0)


def gather_blocks(block_value, axis_name, groups):
    spread = jnp.broadcast_to(block_value[None], (groups,) + block_value.shape)
    collected = lax.all_to_all(spread, axis_name, split_axis=0, concat_axis=0, tiled=True)
    return collected.reshape((groups * block_value.shape[0],) + block_value.shape[1:])


def head_sum_kernel(heads_ref, weight_ref, out_ref):
    total = jnp.zeros(out_ref.shape, jnp.float32)
    for head in range(heads_ref.shape[0]):
        term = jnp.dot(heads_ref[head], weight_ref[head], preferred_element_type=jnp.float32)
        total = total + term.astype(jnp.bfloat16).astype(jnp.float32)
    out_ref[...] = total


def head_sum(heads, weight):
    count, rows, width = heads.shape
    columns = weight.shape[2]
    steps = 2
    tile = rows // steps
    return pl.pallas_call(
        head_sum_kernel,
        grid=(steps,),
        in_specs=[
            pl.BlockSpec((count, tile, width), lambda i: (0, i, 0)),
            pl.BlockSpec((count, width, columns), lambda i: (0, 0, 0)),
        ],
        out_specs=pl.BlockSpec((tile, columns), lambda i: (i, 0)),
        out_shape=jax.ShapeDtypeStruct((rows, columns), jnp.float32),
    )(heads, weight)


def pair_up(value, core, swap, axis):
    other = lax.ppermute(value, "core", swap)
    low = jnp.where(core == 0, value, other)
    high = jnp.where(core == 0, other, value)
    return jnp.concatenate([low, high], axis=axis)


def body(tokens, norm_gain, qkv_weight, qk_gain, out_weight, layer_scale, tile_counts, owners):
    own_rows = tokens[0]
    chips = lax.axis_size("chip")
    cores = lax.axis_size("core")
    groups = chips * cores
    chip = lax.axis_index("chip")
    core = lax.axis_index("core")
    row_index = lax.axis_index("fsdp")
    row_count = lax.axis_size("fsdp")
    model_width = own_rows.shape[1]
    block = model_width // groups
    swap = [(0, 1), (1, 0)]
    spread = jnp.broadcast_to(out_weight[None], (row_count,) + out_weight.shape)
    head_rows = lax.all_to_all(spread, "fsdp", split_axis=0, concat_axis=0, tiled=True)
    per_row = out_weight.shape[1] // block
    head_rows = head_rows.reshape(row_count, HEAD_DIM, per_row, block).transpose(0, 2, 1, 3)
    weight_block = lax.all_to_all(
        head_rows.reshape(groups, HEAD_DIM, block),
        ("chip", "core"),
        split_axis=0,
        concat_axis=0,
        tiled=True,
    ).reshape(groups * HEAD_DIM, block)
    pair_weight = pair_up(weight_block, core, swap, 1)
    full_qkv = gather_blocks(qkv_weight, "fsdp", row_count)
    pair_qkv = pair_up(full_qkv, core, swap, 1)
    pair_qkv, pair_weight = lax.optimization_barrier((pair_qkv, pair_weight))
    pair_gain = pair_up(qk_gain, core, swap, 1).reshape(2, cores, HEAD_DIM)
    half = lax.all_gather(own_rows, "chip", axis=0, tiled=True)
    half_length = half.shape[0]
    piece = own_rows.shape[0]
    values = half.astype(jnp.float32)
    normed = (
        values * lax.rsqrt(jnp.mean(values * values, axis=-1, keepdims=True) + EPSILON) * norm_gain
    ).astype(jnp.bfloat16)
    projected = jnp.dot(normed, pair_qkv, preferred_element_type=jnp.float32)
    projected = projected.reshape(half_length, cores, 3, HEAD_DIM)
    queries = projected[:, :, 0]
    keys_part = projected[:, :, 1]
    values_part = projected[:, :, 2].astype(jnp.bfloat16)
    sums = gather_sum(
        jnp.stack(
            [jnp.sum(queries * queries, axis=(1, 2)), jnp.sum(keys_part * keys_part, axis=(1, 2))]
        ),
        "chip",
        chips,
    )
    window = groups * HEAD_DIM
    queries = (
        queries * lax.rsqrt(sums[0] / window + EPSILON)[:, None, None] * pair_gain[0][None]
    ).astype(jnp.bfloat16)
    keys_part = (
        keys_part * lax.rsqrt(sums[1] / window + EPSILON)[:, None, None] * pair_gain[1][None]
    ).astype(jnp.bfloat16)
    stacked = jnp.stack([queries, keys_part, values_part])
    mine = lax.dynamic_index_in_dim(stacked, core, axis=2, keepdims=False)
    theirs = lax.dynamic_index_in_dim(stacked, 1 - core, axis=2, keepdims=False)
    got = lax.ppermute(theirs, "core", swap)
    first_half = jnp.where(core == 0, mine, got).reshape(3, chips, piece, HEAD_DIM)
    second_half = jnp.where(core == 0, got, mine).reshape(3, chips, piece, HEAD_DIM)
    whole = jnp.stack([first_half, second_half], axis=2).reshape(3, groups * piece, HEAD_DIM)
    length = whole.shape[1]
    factor = HEAD_DIM ** (-0.5)
    covered = SLOTS * TILE
    tile_query = whole[0, :covered].reshape(SLOTS, TILE, HEAD_DIM)
    tile_key = whole[1, :covered].reshape(SLOTS, TILE, HEAD_DIM)
    tile_value = whole[2, :covered].reshape(SLOTS, TILE, HEAD_DIM)
    scores = (
        jnp.einsum("sqc,skc->sqk", tile_query, tile_key, preferred_element_type=jnp.float32)
        * factor
    )
    highest = jnp.max(scores, axis=-1, keepdims=True)
    exponent = jnp.exp(scores - highest)
    weights = (exponent / jnp.sum(exponent, axis=-1, keepdims=True)).astype(jnp.bfloat16)
    tile_out = jnp.einsum(
        "sqk,skc->sqc", weights, tile_value, preferred_element_type=jnp.float32
    ).astype(jnp.bfloat16)
    head_out = jnp.concatenate(
        [
            tile_out.reshape(covered, HEAD_DIM),
            jnp.zeros((length - covered, HEAD_DIM), jnp.bfloat16),
        ],
        axis=0,
    )
    by_half = head_out.reshape(chips, cores, piece, HEAD_DIM).transpose(1, 0, 2, 3)
    by_half = by_half.reshape(cores, half_length, HEAD_DIM)
    outgoing = jnp.broadcast_to(by_half[None], (chips, cores, half_length, HEAD_DIM))
    all_heads = lax.all_to_all(
        outgoing.reshape(groups, half_length, HEAD_DIM),
        ("chip", "core"),
        split_axis=0,
        concat_axis=0,
        tiled=True,
    )
    attention = head_sum(all_heads, pair_weight.reshape(groups, HEAD_DIM, cores * block))
    pair_tokens = lax.dynamic_slice_in_dim(half, chip * cores * block, cores * block, axis=1)
    pair_scale = lax.dynamic_slice_in_dim(layer_scale, chip * cores * block, cores * block)
    updated_half = (pair_tokens.astype(jnp.float32) + pair_scale * attention).astype(jnp.bfloat16)
    keep = lax.dynamic_slice_in_dim(updated_half, core * block, block, axis=1)
    give = lax.dynamic_slice_in_dim(updated_half, (1 - core) * block, block, axis=1)
    taken = lax.ppermute(give, "core", swap)
    first_half = jnp.where(core == 0, keep, taken).reshape(chips, piece, block)
    second_half = jnp.where(core == 0, taken, keep).reshape(chips, piece, block)
    updated = jnp.stack([first_half, second_half], axis=1).reshape(length, block)
    merged = merge_tiles(updated)
    holder, living = tile_owners(tile_counts, owners)
    own_holder = holder[row_index]
    own_living = living[row_index]
    destination = jnp.arange(row_count, dtype=jnp.int32)[:, None]
    sending = jnp.logical_and(destination == own_holder[None, :], own_living[None, :])
    outgoing = jnp.where(sending[:, :, None, None], merged[None], jnp.zeros((), jnp.bfloat16))
    received = lax.all_to_all(outgoing, "fsdp", split_axis=0, concat_axis=0, tiled=True)
    return place_tiles(received, holder, living, row_index)


def solution(mesh):
    fsdp_size = mesh.shape["fsdp"]
    dp_size = mesh.shape["dp"]
    split = Mesh(
        mesh.devices.reshape(fsdp_size, dp_size // 2, 2), ("fsdp", "chip", "core")
    )
    heads = ("chip", "core")
    placed = (
        P("fsdp", heads, None),
        P(),
        P("fsdp", heads),
        P(None, heads),
        P(heads, "fsdp"),
        P(),
        P(),
        P(),
    )
    return jax.shard_map(
        body, mesh=split, in_specs=placed, out_specs=P("fsdp", None, heads), check_vma=False
    )
```

```python
import jax
import jax.numpy as jnp
from jax import lax
from jax.experimental import pallas as pl
from jax.sharding import Mesh, PartitionSpec as P

HEAD_DIM = 128
GRID = 32
SLOTS = 2
TILE = 1025
CAP = 4


EPSILON = 1e-06


def merge_tiles(values):
    halves = GRID // 2
    columns = values.shape[1]
    tile_list = []
    for tile_slot in range(SLOTS):
        patches = values[tile_slot * TILE + 1 : (tile_slot + 1) * TILE]
        square = patches.reshape(halves, 2, halves, 2, columns).transpose(0, 2, 4, 1, 3)
        tile_list.append(square.reshape(halves * halves, columns * 4))
    return jnp.stack(tile_list)


def tile_owners(tile_counts, owners):
    slot_index = jnp.arange(SLOTS, dtype=jnp.int32)[None, :]
    first_count = tile_counts[:, 0:1]
    holder = jnp.where(slot_index < first_count, owners[:, 0:1], owners[:, 1:2])
    living = slot_index < first_count + tile_counts[:, 1:2]
    return (holder, living)


def place_tiles(received, holder, living, target):
    owned_flag = jnp.logical_and(living, holder == target).reshape(-1).astype(jnp.int32)
    before = jnp.cumsum(owned_flag) - owned_flag
    flattened = received.reshape((received.shape[0] * received.shape[1],) + received.shape[2:])
    sources = jnp.arange(flattened.shape[0], dtype=jnp.int32)
    placed = []
    for slot in range(CAP):
        match = jnp.logical_and(before == slot, owned_flag == 1)
        source = jnp.max(jnp.where(match, sources, 0))
        tile = lax.dynamic_index_in_dim(flattened, source, axis=0, keepdims=False)
        placed.append(jnp.where(jnp.any(match), tile, jnp.zeros((), tile.dtype)))
    return jnp.stack(placed)


def gather_sum(values, axis_name, groups):
    spread = jnp.broadcast_to(values[None], (groups,) + values.shape)
    collected = lax.all_to_all(spread, axis_name, split_axis=0, concat_axis=0, tiled=True)
    return jnp.sum(collected, axis=0)


def gather_blocks(block_value, axis_name, groups):
    spread = jnp.broadcast_to(block_value[None], (groups,) + block_value.shape)
    collected = lax.all_to_all(spread, axis_name, split_axis=0, concat_axis=0, tiled=True)
    return collected.reshape((groups * block_value.shape[0],) + block_value.shape[1:])


def head_sum_kernel(heads_ref, weight_ref, out_ref):
    total = jnp.zeros(out_ref.shape, jnp.float32)
    for head in range(heads_ref.shape[0]):
        term = jnp.dot(heads_ref[head], weight_ref[head], preferred_element_type=jnp.float32)
        total = total + term.astype(jnp.bfloat16).astype(jnp.float32)
    out_ref[...] = total


def head_sum(heads, weight):
    count, rows, width = heads.shape
    columns = weight.shape[2]
    steps = 4
    tile = rows // steps
    return pl.pallas_call(
        head_sum_kernel,
        grid=(steps,),
        in_specs=[
            pl.BlockSpec((count, tile, width), lambda i: (0, i, 0)),
            pl.BlockSpec((count, width, columns), lambda i: (0, 0, 0)),
        ],
        out_specs=pl.BlockSpec((tile, columns), lambda i: (i, 0)),
        out_shape=jax.ShapeDtypeStruct((rows, columns), jnp.float32),
    )(heads, weight)


def pair_up(value, core, swap, axis):
    other = lax.ppermute(value, "core", swap)
    low = jnp.where(core == 0, value, other)
    high = jnp.where(core == 0, other, value)
    return jnp.concatenate([low, high], axis=axis)


def body(tokens, norm_gain, qkv_weight, qk_gain, out_weight, layer_scale, tile_counts, owners):
    own_rows = tokens[0]
    chips = lax.axis_size("chip")
    cores = lax.axis_size("core")
    groups = chips * cores
    chip = lax.axis_index("chip")
    core = lax.axis_index("core")
    row_index = lax.axis_index("fsdp")
    row_count = lax.axis_size("fsdp")
    model_width = own_rows.shape[1]
    block = model_width // groups
    swap = [(0, 1), (1, 0)]
    spread = jnp.broadcast_to(out_weight[None], (row_count,) + out_weight.shape)
    head_rows = lax.all_to_all(spread, "fsdp", split_axis=0, concat_axis=0, tiled=True)
    per_row = out_weight.shape[1] // block
    head_rows = head_rows.reshape(row_count, HEAD_DIM, per_row, block).transpose(0, 2, 1, 3)
    weight_block = lax.all_to_all(
        head_rows.reshape(groups, HEAD_DIM, block),
        ("chip", "core"),
        split_axis=0,
        concat_axis=0,
        tiled=True,
    ).reshape(groups * HEAD_DIM, block)
    pair_weight = pair_up(weight_block, core, swap, 1)
    full_qkv = gather_blocks(qkv_weight, "fsdp", row_count)
    pair_qkv = pair_up(full_qkv, core, swap, 1)
    pair_qkv, pair_weight = lax.optimization_barrier((pair_qkv, pair_weight))
    pair_gain = pair_up(qk_gain, core, swap, 1).reshape(2, cores, HEAD_DIM)
    half = lax.all_gather(own_rows, "chip", axis=0, tiled=True)
    half_length = half.shape[0]
    piece = own_rows.shape[0]
    values = half.astype(jnp.float32)
    normed = (
        values * lax.rsqrt(jnp.mean(values * values, axis=-1, keepdims=True) + EPSILON) * norm_gain
    ).astype(jnp.bfloat16)
    projected = jnp.dot(normed, pair_qkv, preferred_element_type=jnp.float32)
    projected = projected.reshape(half_length, cores, 3, HEAD_DIM)
    queries = projected[:, :, 0]
    keys_part = projected[:, :, 1]
    values_part = projected[:, :, 2].astype(jnp.bfloat16)
    sums = gather_sum(
        jnp.stack(
            [jnp.sum(queries * queries, axis=(1, 2)), jnp.sum(keys_part * keys_part, axis=(1, 2))]
        ),
        "chip",
        chips,
    )
    window = groups * HEAD_DIM
    queries = (
        queries * lax.rsqrt(sums[0] / window + EPSILON)[:, None, None] * pair_gain[0][None]
    ).astype(jnp.bfloat16)
    keys_part = (
        keys_part * lax.rsqrt(sums[1] / window + EPSILON)[:, None, None] * pair_gain[1][None]
    ).astype(jnp.bfloat16)
    stacked = jnp.stack([queries, keys_part, values_part])
    mine = lax.dynamic_index_in_dim(stacked, core, axis=2, keepdims=False)
    theirs = lax.dynamic_index_in_dim(stacked, 1 - core, axis=2, keepdims=False)
    got = lax.ppermute(theirs, "core", swap)
    first_half = jnp.where(core == 0, mine, got).reshape(3, chips, piece, HEAD_DIM)
    second_half = jnp.where(core == 0, got, mine).reshape(3, chips, piece, HEAD_DIM)
    whole = jnp.stack([first_half, second_half], axis=2).reshape(3, groups * piece, HEAD_DIM)
    length = whole.shape[1]
    factor = HEAD_DIM ** (-0.5)
    covered = SLOTS * TILE
    tile_query = whole[0, :covered].reshape(SLOTS, TILE, HEAD_DIM)
    tile_key = whole[1, :covered].reshape(SLOTS, TILE, HEAD_DIM)
    tile_value = whole[2, :covered].reshape(SLOTS, TILE, HEAD_DIM)
    scores = (
        jnp.einsum("sqc,skc->sqk", tile_query, tile_key, preferred_element_type=jnp.float32)
        * factor
    )
    highest = jnp.max(scores, axis=-1, keepdims=True)
    exponent = jnp.exp(scores - highest)
    weights = (exponent / jnp.sum(exponent, axis=-1, keepdims=True)).astype(jnp.bfloat16)
    tile_out = jnp.einsum(
        "sqk,skc->sqc", weights, tile_value, preferred_element_type=jnp.float32
    ).astype(jnp.bfloat16)
    head_out = jnp.concatenate(
        [
            tile_out.reshape(covered, HEAD_DIM),
            jnp.zeros((length - covered, HEAD_DIM), jnp.bfloat16),
        ],
        axis=0,
    )
    by_half = head_out.reshape(chips, cores, piece, HEAD_DIM).transpose(1, 0, 2, 3)
    by_half = by_half.reshape(cores, half_length, HEAD_DIM)
    outgoing = jnp.broadcast_to(by_half[None], (chips, cores, half_length, HEAD_DIM))
    all_heads = lax.all_to_all(
        outgoing.reshape(groups, half_length, HEAD_DIM),
        ("chip", "core"),
        split_axis=0,
        concat_axis=0,
        tiled=True,
    )
    attention = head_sum(all_heads, pair_weight.reshape(groups, HEAD_DIM, cores * block))
    pair_tokens = lax.dynamic_slice_in_dim(half, chip * cores * block, cores * block, axis=1)
    pair_scale = lax.dynamic_slice_in_dim(layer_scale, chip * cores * block, cores * block)
    updated_half = (pair_tokens.astype(jnp.float32) + pair_scale * attention).astype(jnp.bfloat16)
    keep = lax.dynamic_slice_in_dim(updated_half, core * block, block, axis=1)
    give = lax.dynamic_slice_in_dim(updated_half, (1 - core) * block, block, axis=1)
    taken = lax.ppermute(give, "core", swap)
    first_half = jnp.where(core == 0, keep, taken).reshape(chips, piece, block)
    second_half = jnp.where(core == 0, taken, keep).reshape(chips, piece, block)
    updated = jnp.stack([first_half, second_half], axis=1).reshape(length, block)
    merged = merge_tiles(updated)
    holder, living = tile_owners(tile_counts, owners)
    own_holder = holder[row_index]
    own_living = living[row_index]
    destination = jnp.arange(row_count, dtype=jnp.int32)[:, None]
    sending = jnp.logical_and(destination == own_holder[None, :], own_living[None, :])
    outgoing = jnp.where(sending[:, :, None, None], merged[None], jnp.zeros((), jnp.bfloat16))
    received = lax.all_to_all(outgoing, "fsdp", split_axis=0, concat_axis=0, tiled=True)
    return place_tiles(received, holder, living, row_index)


def solution(mesh):
    fsdp_size = mesh.shape["fsdp"]
    dp_size = mesh.shape["dp"]
    split = Mesh(
        mesh.devices.reshape(fsdp_size, dp_size // 2, 2), ("fsdp", "chip", "core")
    )
    heads = ("chip", "core")
    placed = (
        P("fsdp", heads, None),
        P(),
        P("fsdp", heads),
        P(None, heads),
        P(heads, "fsdp"),
        P(),
        P(),
        P(),
    )
    return jax.shard_map(
        body, mesh=split, in_specs=placed, out_specs=P("fsdp", None, heads), check_vma=False
    )
```

```python
import jax
import jax.numpy as jnp
from jax import lax
from jax.experimental import pallas as pl
from jax.sharding import Mesh, PartitionSpec as P

HEAD_DIM = 128
GRID = 32
SLOTS = 2
TILE = 1025
CAP = 4


EPSILON = 1e-06


def merge_tiles(values):
    halves = GRID // 2
    columns = values.shape[1]
    tile_list = []
    for tile_slot in range(SLOTS):
        patches = values[tile_slot * TILE + 1 : (tile_slot + 1) * TILE]
        square = patches.reshape(halves, 2, halves, 2, columns).transpose(0, 2, 4, 1, 3)
        tile_list.append(square.reshape(halves * halves, columns * 4))
    return jnp.stack(tile_list)


def tile_owners(tile_counts, owners):
    slot_index = jnp.arange(SLOTS, dtype=jnp.int32)[None, :]
    first_count = tile_counts[:, 0:1]
    holder = jnp.where(slot_index < first_count, owners[:, 0:1], owners[:, 1:2])
    living = slot_index < first_count + tile_counts[:, 1:2]
    return (holder, living)


def place_tiles(received, holder, living, target):
    owned_flag = jnp.logical_and(living, holder == target).reshape(-1).astype(jnp.int32)
    before = jnp.cumsum(owned_flag) - owned_flag
    flattened = received.reshape((received.shape[0] * received.shape[1],) + received.shape[2:])
    sources = jnp.arange(flattened.shape[0], dtype=jnp.int32)
    placed = []
    for slot in range(CAP):
        match = jnp.logical_and(before == slot, owned_flag == 1)
        source = jnp.max(jnp.where(match, sources, 0))
        tile = lax.dynamic_index_in_dim(flattened, source, axis=0, keepdims=False)
        placed.append(jnp.where(jnp.any(match), tile, jnp.zeros((), tile.dtype)))
    return jnp.stack(placed)


def gather_sum(values, axis_name, groups):
    spread = jnp.broadcast_to(values[None], (groups,) + values.shape)
    collected = lax.all_to_all(spread, axis_name, split_axis=0, concat_axis=0, tiled=True)
    return jnp.sum(collected, axis=0)


def gather_blocks(block_value, axis_name, groups):
    spread = jnp.broadcast_to(block_value[None], (groups,) + block_value.shape)
    collected = lax.all_to_all(spread, axis_name, split_axis=0, concat_axis=0, tiled=True)
    return collected.reshape((groups * block_value.shape[0],) + block_value.shape[1:])


def head_sum_kernel(heads_ref, weight_ref, tokens_ref, scale_ref, out_ref):
    total = jnp.zeros(out_ref.shape, jnp.float32)
    for head in range(heads_ref.shape[0]):
        term = jnp.dot(heads_ref[head], weight_ref[head], preferred_element_type=jnp.float32)
        total = total + term.astype(jnp.bfloat16).astype(jnp.float32)
    updated = tokens_ref[...].astype(jnp.float32) + scale_ref[...] * total
    out_ref[...] = updated.astype(out_ref.dtype)


def head_sum(heads, weight, tokens, scale):
    count, rows, width = heads.shape
    columns = weight.shape[2]
    steps = 4
    tile = rows // steps
    return pl.pallas_call(
        head_sum_kernel,
        grid=(steps,),
        in_specs=[
            pl.BlockSpec((count, tile, width), lambda i: (0, i, 0)),
            pl.BlockSpec((count, width, columns), lambda i: (0, 0, 0)),
            pl.BlockSpec((tile, columns), lambda i: (i, 0)),
            pl.BlockSpec((1, columns), lambda i: (0, 0)),
        ],
        out_specs=pl.BlockSpec((tile, columns), lambda i: (i, 0)),
        out_shape=jax.ShapeDtypeStruct((rows, columns), tokens.dtype),
    )(heads, weight, tokens, scale.reshape(1, columns))


def pair_up(value, core, swap, axis):
    other = lax.ppermute(value, "core", swap)
    low = jnp.where(core == 0, value, other)
    high = jnp.where(core == 0, other, value)
    return jnp.concatenate([low, high], axis=axis)


def body(tokens, norm_gain, qkv_weight, qk_gain, out_weight, layer_scale, tile_counts, owners):
    own_rows = tokens[0]
    chips = lax.axis_size("chip")
    cores = lax.axis_size("core")
    groups = chips * cores
    chip = lax.axis_index("chip")
    core = lax.axis_index("core")
    row_index = lax.axis_index("fsdp")
    row_count = lax.axis_size("fsdp")
    model_width = own_rows.shape[1]
    block = model_width // groups
    swap = [(0, 1), (1, 0)]
    spread = jnp.broadcast_to(out_weight[None], (row_count,) + out_weight.shape)
    head_rows = lax.all_to_all(spread, "fsdp", split_axis=0, concat_axis=0, tiled=True)
    per_row = out_weight.shape[1] // block
    head_rows = head_rows.reshape(row_count, HEAD_DIM, per_row, block).transpose(0, 2, 1, 3)
    weight_block = lax.all_to_all(
        head_rows.reshape(groups, HEAD_DIM, block),
        ("chip", "core"),
        split_axis=0,
        concat_axis=0,
        tiled=True,
    ).reshape(groups * HEAD_DIM, block)
    pair_weight = pair_up(weight_block, core, swap, 1)
    full_qkv = gather_blocks(qkv_weight, "fsdp", row_count)
    pair_qkv = pair_up(full_qkv, core, swap, 1)
    pair_qkv, pair_weight = lax.optimization_barrier((pair_qkv, pair_weight))
    pair_gain = pair_up(qk_gain, core, swap, 1).reshape(2, cores, HEAD_DIM)
    half = lax.all_gather(own_rows, "chip", axis=0, tiled=True)
    half_length = half.shape[0]
    piece = own_rows.shape[0]
    values = half.astype(jnp.float32)
    normed = (
        values * lax.rsqrt(jnp.mean(values * values, axis=-1, keepdims=True) + EPSILON) * norm_gain
    ).astype(jnp.bfloat16)
    projected = jnp.dot(normed, pair_qkv, preferred_element_type=jnp.float32)
    projected = projected.reshape(half_length, cores, 3, HEAD_DIM)
    queries = projected[:, :, 0]
    keys_part = projected[:, :, 1]
    values_part = projected[:, :, 2].astype(jnp.bfloat16)
    sums = gather_sum(
        jnp.stack(
            [jnp.sum(queries * queries, axis=(1, 2)), jnp.sum(keys_part * keys_part, axis=(1, 2))]
        ),
        "chip",
        chips,
    )
    window = groups * HEAD_DIM
    queries = (
        queries * lax.rsqrt(sums[0] / window + EPSILON)[:, None, None] * pair_gain[0][None]
    ).astype(jnp.bfloat16)
    keys_part = (
        keys_part * lax.rsqrt(sums[1] / window + EPSILON)[:, None, None] * pair_gain[1][None]
    ).astype(jnp.bfloat16)
    stacked = jnp.stack([queries, keys_part, values_part])
    mine = lax.dynamic_index_in_dim(stacked, core, axis=2, keepdims=False)
    theirs = lax.dynamic_index_in_dim(stacked, 1 - core, axis=2, keepdims=False)
    got = lax.ppermute(theirs, "core", swap)
    first_half = jnp.where(core == 0, mine, got).reshape(3, chips, piece, HEAD_DIM)
    second_half = jnp.where(core == 0, got, mine).reshape(3, chips, piece, HEAD_DIM)
    whole = jnp.stack([first_half, second_half], axis=2).reshape(3, groups * piece, HEAD_DIM)
    length = whole.shape[1]
    factor = HEAD_DIM ** (-0.5)
    covered = SLOTS * TILE
    tile_query = whole[0, :covered].reshape(SLOTS, TILE, HEAD_DIM)
    tile_key = whole[1, :covered].reshape(SLOTS, TILE, HEAD_DIM)
    tile_value = whole[2, :covered].reshape(SLOTS, TILE, HEAD_DIM)
    scores = (
        jnp.einsum("sqc,skc->sqk", tile_query, tile_key, preferred_element_type=jnp.float32)
        * factor
    )
    highest = jnp.max(scores, axis=-1, keepdims=True)
    exponent = jnp.exp(scores - highest)
    weights = (exponent / jnp.sum(exponent, axis=-1, keepdims=True)).astype(jnp.bfloat16)
    tile_out = jnp.einsum(
        "sqk,skc->sqc", weights, tile_value, preferred_element_type=jnp.float32
    ).astype(jnp.bfloat16)
    head_out = jnp.concatenate(
        [
            tile_out.reshape(covered, HEAD_DIM),
            jnp.zeros((length - covered, HEAD_DIM), jnp.bfloat16),
        ],
        axis=0,
    )
    by_half = head_out.reshape(chips, cores, piece, HEAD_DIM).transpose(1, 0, 2, 3)
    by_half = by_half.reshape(cores, half_length, HEAD_DIM)
    outgoing = jnp.broadcast_to(by_half[None], (chips, cores, half_length, HEAD_DIM))
    all_heads = lax.all_to_all(
        outgoing.reshape(groups, half_length, HEAD_DIM),
        ("chip", "core"),
        split_axis=0,
        concat_axis=0,
        tiled=True,
    )
    pair_tokens = lax.dynamic_slice_in_dim(half, chip * cores * block, cores * block, axis=1)
    pair_scale = lax.dynamic_slice_in_dim(layer_scale, chip * cores * block, cores * block)
    updated_half = head_sum(
        all_heads, pair_weight.reshape(groups, HEAD_DIM, cores * block), pair_tokens, pair_scale
    )
    keep = lax.dynamic_slice_in_dim(updated_half, core * block, block, axis=1)
    give = lax.dynamic_slice_in_dim(updated_half, (1 - core) * block, block, axis=1)
    taken = lax.ppermute(give, "core", swap)
    first_half = jnp.where(core == 0, keep, taken).reshape(chips, piece, block)
    second_half = jnp.where(core == 0, taken, keep).reshape(chips, piece, block)
    updated = jnp.stack([first_half, second_half], axis=1).reshape(length, block)
    merged = merge_tiles(updated)
    holder, living = tile_owners(tile_counts, owners)
    own_holder = holder[row_index]
    own_living = living[row_index]
    destination = jnp.arange(row_count, dtype=jnp.int32)[:, None]
    sending = jnp.logical_and(destination == own_holder[None, :], own_living[None, :])
    outgoing = jnp.where(sending[:, :, None, None], merged[None], jnp.zeros((), jnp.bfloat16))
    received = lax.all_to_all(outgoing, "fsdp", split_axis=0, concat_axis=0, tiled=True)
    return place_tiles(received, holder, living, row_index)


def solution(mesh):
    fsdp_size = mesh.shape["fsdp"]
    dp_size = mesh.shape["dp"]
    split = Mesh(
        mesh.devices.reshape(fsdp_size, dp_size // 2, 2), ("fsdp", "chip", "core")
    )
    heads = ("chip", "core")
    placed = (
        P("fsdp", heads, None),
        P(),
        P("fsdp", heads),
        P(None, heads),
        P(heads, "fsdp"),
        P(),
        P(),
        P(),
    )
    return jax.shard_map(
        body, mesh=split, in_specs=placed, out_specs=P("fsdp", None, heads), check_vma=False
    )
```

```python
import jax
import jax.numpy as jnp
from jax import lax
from jax.experimental import pallas as pl
from jax.sharding import Mesh, PartitionSpec as P

HEAD_DIM = 128
GRID = 32
SLOTS = 2
TILE = 1025
CAP = 4


EPSILON = 1e-06


def merge_tiles(values):
    halves = GRID // 2
    columns = values.shape[1]
    tile_list = []
    for tile_slot in range(SLOTS):
        patches = values[tile_slot * TILE + 1 : (tile_slot + 1) * TILE]
        square = patches.reshape(halves, 2, halves, 2, columns).transpose(0, 2, 4, 1, 3)
        tile_list.append(square.reshape(halves * halves, columns * 4))
    return jnp.stack(tile_list)


def tile_owners(tile_counts, owners):
    slot_index = jnp.arange(SLOTS, dtype=jnp.int32)[None, :]
    first_count = tile_counts[:, 0:1]
    holder = jnp.where(slot_index < first_count, owners[:, 0:1], owners[:, 1:2])
    living = slot_index < first_count + tile_counts[:, 1:2]
    return (holder, living)


def place_tiles(received, holder, living, target):
    owned_flag = jnp.logical_and(living, holder == target).reshape(-1).astype(jnp.int32)
    before = jnp.cumsum(owned_flag) - owned_flag
    flattened = received.reshape((received.shape[0] * received.shape[1],) + received.shape[2:])
    sources = jnp.arange(flattened.shape[0], dtype=jnp.int32)
    placed = []
    for slot in range(CAP):
        match = jnp.logical_and(before == slot, owned_flag == 1)
        source = jnp.max(jnp.where(match, sources, 0))
        tile = lax.dynamic_index_in_dim(flattened, source, axis=0, keepdims=False)
        placed.append(jnp.where(jnp.any(match), tile, jnp.zeros((), tile.dtype)))
    return jnp.stack(placed)


def gather_sum(values, axis_name, groups):
    spread = jnp.broadcast_to(values[None], (groups,) + values.shape)
    collected = lax.all_to_all(spread, axis_name, split_axis=0, concat_axis=0, tiled=True)
    return jnp.sum(collected, axis=0)


def gather_blocks(block_value, axis_name, groups):
    spread = jnp.broadcast_to(block_value[None], (groups,) + block_value.shape)
    collected = lax.all_to_all(spread, axis_name, split_axis=0, concat_axis=0, tiled=True)
    return collected.reshape((groups * block_value.shape[0],) + block_value.shape[1:])


def head_sum_kernel(heads_ref, weight_ref, tokens_ref, scale_ref, out_ref):
    total = jnp.zeros(out_ref.shape, jnp.float32)
    for head in range(heads_ref.shape[0]):
        term = jnp.dot(heads_ref[head], weight_ref[head], preferred_element_type=jnp.float32)
        total = total + term.astype(jnp.bfloat16).astype(jnp.float32)
    updated = tokens_ref[...].astype(jnp.float32) + scale_ref[...] * total
    out_ref[...] = updated.astype(out_ref.dtype)


def head_sum(heads, weight, tokens, scale):
    count, rows, width = heads.shape
    columns = weight.shape[2]
    steps = 4
    tile = rows // steps
    return pl.pallas_call(
        head_sum_kernel,
        grid=(steps,),
        in_specs=[
            pl.BlockSpec((count, tile, width), lambda i: (0, i, 0)),
            pl.BlockSpec((count, width, columns), lambda i: (0, 0, 0)),
            pl.BlockSpec((tile, columns), lambda i: (i, 0)),
            pl.BlockSpec((1, columns), lambda i: (0, 0)),
        ],
        out_specs=pl.BlockSpec((tile, columns), lambda i: (i, 0)),
        out_shape=jax.ShapeDtypeStruct((rows, columns), tokens.dtype),
    )(heads, weight, tokens, scale.reshape(1, columns))


def pair_up(value, core, swap, axis):
    other = lax.ppermute(value, "core", swap)
    low = jnp.where(core == 0, value, other)
    high = jnp.where(core == 0, other, value)
    return jnp.concatenate([low, high], axis=axis)


def body(tokens, norm_gain, qkv_weight, qk_gain, out_weight, layer_scale, tile_counts, owners):
    own_rows = tokens[0]
    chips = lax.axis_size("chip")
    cores = lax.axis_size("core")
    groups = chips * cores
    chip = lax.axis_index("chip")
    core = lax.axis_index("core")
    row_index = lax.axis_index("fsdp")
    row_count = lax.axis_size("fsdp")
    model_width = own_rows.shape[1]
    block = model_width // groups
    swap = [(0, 1), (1, 0)]
    spread = jnp.broadcast_to(out_weight[None], (row_count,) + out_weight.shape)
    head_rows = lax.all_to_all(spread, "fsdp", split_axis=0, concat_axis=0, tiled=True)
    per_row = out_weight.shape[1] // block
    head_rows = head_rows.reshape(row_count, HEAD_DIM, per_row, block).transpose(0, 2, 1, 3)
    weight_block = lax.all_to_all(
        head_rows.reshape(groups, HEAD_DIM, block),
        ("chip", "core"),
        split_axis=0,
        concat_axis=0,
        tiled=True,
    ).reshape(groups * HEAD_DIM, block)
    pair_weight = pair_up(weight_block, core, swap, 1)
    full_qkv = gather_blocks(qkv_weight, "fsdp", row_count)
    pair_qkv = pair_up(full_qkv, core, swap, 1)
    pair_qkv, pair_weight = lax.optimization_barrier((pair_qkv, pair_weight))
    pair_gain = pair_up(qk_gain, core, swap, 1).reshape(2, cores, HEAD_DIM)
    half = lax.all_gather(own_rows, "chip", axis=0, tiled=True)
    half_length = half.shape[0]
    piece = own_rows.shape[0]
    values = half.astype(jnp.float32)
    normed = (
        values * lax.rsqrt(jnp.mean(values * values, axis=-1, keepdims=True) + EPSILON) * norm_gain
    ).astype(jnp.bfloat16)
    projected = jnp.dot(normed, pair_qkv, preferred_element_type=jnp.float32)
    projected = projected.reshape(half_length, cores, 3, HEAD_DIM)
    queries = projected[:, :, 0]
    keys_part = projected[:, :, 1]
    values_part = projected[:, :, 2].astype(jnp.bfloat16)
    sums = gather_sum(
        jnp.stack(
            [jnp.sum(queries * queries, axis=(1, 2)), jnp.sum(keys_part * keys_part, axis=(1, 2))]
        ),
        "chip",
        chips,
    )
    window = groups * HEAD_DIM
    queries = (
        queries * lax.rsqrt(sums[0] / window + EPSILON)[:, None, None] * pair_gain[0][None]
    ).astype(jnp.bfloat16)
    keys_part = (
        keys_part * lax.rsqrt(sums[1] / window + EPSILON)[:, None, None] * pair_gain[1][None]
    ).astype(jnp.bfloat16)
    stacked = jnp.stack([queries, keys_part, values_part])
    mine = lax.dynamic_index_in_dim(stacked, core, axis=2, keepdims=False)
    theirs = lax.dynamic_index_in_dim(stacked, 1 - core, axis=2, keepdims=False)
    got = lax.ppermute(theirs, "core", swap)
    first_half = jnp.where(core == 0, mine, got).reshape(3, chips, piece, HEAD_DIM)
    second_half = jnp.where(core == 0, got, mine).reshape(3, chips, piece, HEAD_DIM)
    whole = jnp.stack([first_half, second_half], axis=2).reshape(3, groups * piece, HEAD_DIM)
    length = whole.shape[1]
    factor = HEAD_DIM ** (-0.5)
    covered = SLOTS * TILE
    tile_query = whole[0, :covered].reshape(SLOTS, TILE, HEAD_DIM)
    tile_key = whole[1, :covered].reshape(SLOTS, TILE, HEAD_DIM)
    tile_value = whole[2, :covered].reshape(SLOTS, TILE, HEAD_DIM)
    scores = (
        jnp.einsum("sqc,skc->sqk", tile_query, tile_key, preferred_element_type=jnp.float32)
        * factor
    )
    highest = jnp.max(scores, axis=-1, keepdims=True)
    exponent = jnp.exp(scores - highest)
    weights = (exponent / jnp.sum(exponent, axis=-1, keepdims=True)).astype(jnp.bfloat16)
    tile_out = jnp.einsum(
        "sqk,skc->sqc", weights, tile_value, preferred_element_type=jnp.float32
    ).astype(jnp.bfloat16)
    head_out = jnp.concatenate(
        [
            tile_out.reshape(covered, HEAD_DIM),
            jnp.zeros((length - covered, HEAD_DIM), jnp.bfloat16),
        ],
        axis=0,
    )
    by_half = head_out.reshape(chips, cores, piece, HEAD_DIM).transpose(1, 0, 2, 3)
    by_half = by_half.reshape(cores, half_length, HEAD_DIM)
    outgoing = jnp.broadcast_to(by_half[None], (chips, cores, half_length, HEAD_DIM))
    all_heads = lax.all_to_all(
        outgoing.reshape(groups, half_length, HEAD_DIM),
        ("chip", "core"),
        split_axis=0,
        concat_axis=0,
        tiled=True,
    )
    pair_tokens = lax.dynamic_slice_in_dim(half, chip * cores * block, cores * block, axis=1)
    pair_scale = lax.dynamic_slice_in_dim(layer_scale, chip * cores * block, cores * block)
    updated_half = head_sum(
        all_heads, pair_weight.reshape(groups, HEAD_DIM, cores * block), pair_tokens, pair_scale
    )
    keep = lax.dynamic_slice_in_dim(updated_half, core * block, block, axis=1)
    give = lax.dynamic_slice_in_dim(updated_half, (1 - core) * block, block, axis=1)
    taken = lax.ppermute(give, "core", swap)
    first_half = jnp.where(core == 0, keep, taken).reshape(chips, piece, block)
    second_half = jnp.where(core == 0, taken, keep).reshape(chips, piece, block)
    updated = jnp.stack([first_half, second_half], axis=1).reshape(length, block)
    patches = jnp.stack([updated[slot * TILE + 1 : (slot + 1) * TILE] for slot in range(SLOTS)])
    halves = GRID // 2
    square = patches.reshape(SLOTS, halves, 2, halves, 2, block).transpose(0, 1, 3, 5, 2, 4)
    merged = square.reshape(SLOTS, halves * halves, block * 4)
    holder, living = tile_owners(tile_counts, owners)
    own_holder = holder[row_index]
    own_living = living[row_index]
    destination = jnp.arange(row_count, dtype=jnp.int32)[:, None]
    sending = jnp.logical_and(destination == own_holder[None, :], own_living[None, :])
    outgoing = jnp.where(sending[:, :, None, None], merged[None], jnp.zeros((), jnp.bfloat16))
    received = lax.all_to_all(outgoing, "fsdp", split_axis=0, concat_axis=0, tiled=True)
    return place_tiles(received, holder, living, row_index)


def solution(mesh):
    fsdp_size = mesh.shape["fsdp"]
    dp_size = mesh.shape["dp"]
    split = Mesh(
        mesh.devices.reshape(fsdp_size, dp_size // 2, 2), ("fsdp", "chip", "core")
    )
    heads = ("chip", "core")
    placed = (
        P("fsdp", heads, None),
        P(),
        P("fsdp", heads),
        P(None, heads),
        P(heads, "fsdp"),
        P(),
        P(),
        P(),
    )
    return jax.shard_map(
        body, mesh=split, in_specs=placed, out_specs=P("fsdp", None, heads), check_vma=False
    )
```

```python
import jax
import jax.numpy as jnp
from jax import lax
from jax.experimental import pallas as pl
from jax.sharding import Mesh, PartitionSpec as P

HEAD_DIM = 128
GRID = 32
SLOTS = 2
TILE = 1025
CAP = 4


EPSILON = 1e-06


def merge_tiles(values):
    halves = GRID // 2
    columns = values.shape[1]
    tile_list = []
    for tile_slot in range(SLOTS):
        patches = values[tile_slot * TILE + 1 : (tile_slot + 1) * TILE]
        square = patches.reshape(halves, 2, halves, 2, columns).transpose(0, 2, 4, 1, 3)
        tile_list.append(square.reshape(halves * halves, columns * 4))
    return jnp.stack(tile_list)


def tile_owners(tile_counts, owners):
    slot_index = jnp.arange(SLOTS, dtype=jnp.int32)[None, :]
    first_count = tile_counts[:, 0:1]
    holder = jnp.where(slot_index < first_count, owners[:, 0:1], owners[:, 1:2])
    living = slot_index < first_count + tile_counts[:, 1:2]
    return (holder, living)


def place_tiles(received, holder, living, target):
    owned_flag = jnp.logical_and(living, holder == target).reshape(-1).astype(jnp.int32)
    before = jnp.cumsum(owned_flag) - owned_flag
    flattened = received.reshape((received.shape[0] * received.shape[1],) + received.shape[2:])
    sources = jnp.arange(flattened.shape[0], dtype=jnp.int32)
    placed = []
    for slot in range(CAP):
        match = jnp.logical_and(before == slot, owned_flag == 1)
        source = jnp.max(jnp.where(match, sources, 0))
        tile = lax.dynamic_index_in_dim(flattened, source, axis=0, keepdims=False)
        placed.append(jnp.where(jnp.any(match), tile, jnp.zeros((), tile.dtype)))
    return jnp.stack(placed)


def gather_sum(values, axis_name, groups):
    spread = jnp.broadcast_to(values[None], (groups,) + values.shape)
    collected = lax.all_to_all(spread, axis_name, split_axis=0, concat_axis=0, tiled=True)
    return jnp.sum(collected, axis=0)


def gather_blocks(block_value, axis_name, groups):
    spread = jnp.broadcast_to(block_value[None], (groups,) + block_value.shape)
    collected = lax.all_to_all(spread, axis_name, split_axis=0, concat_axis=0, tiled=True)
    return collected.reshape((groups * block_value.shape[0],) + block_value.shape[1:])


def head_sum_kernel(heads_ref, weight_ref, tokens_ref, scale_ref, out_ref):
    total = jnp.zeros(out_ref.shape, jnp.float32)
    for head in range(heads_ref.shape[0]):
        term = jnp.dot(heads_ref[head], weight_ref[head], preferred_element_type=jnp.float32)
        total = total + term.astype(jnp.bfloat16).astype(jnp.float32)
    updated = tokens_ref[...].astype(jnp.float32) + scale_ref[...] * total
    out_ref[...] = updated.astype(out_ref.dtype)


def head_sum(heads, weight, tokens, scale):
    count, rows, width = heads.shape
    columns = weight.shape[2]
    steps = 4
    tile = rows // steps
    return pl.pallas_call(
        head_sum_kernel,
        grid=(steps,),
        in_specs=[
            pl.BlockSpec((count, tile, width), lambda i: (0, i, 0)),
            pl.BlockSpec((count, width, columns), lambda i: (0, 0, 0)),
            pl.BlockSpec((tile, columns), lambda i: (i, 0)),
            pl.BlockSpec((1, columns), lambda i: (0, 0)),
        ],
        out_specs=pl.BlockSpec((tile, columns), lambda i: (i, 0)),
        out_shape=jax.ShapeDtypeStruct((rows, columns), tokens.dtype),
    )(heads, weight, tokens, scale.reshape(1, columns))


def pair_up(value, core, swap, axis):
    other = lax.ppermute(value, "core", swap)
    low = jnp.where(core == 0, value, other)
    high = jnp.where(core == 0, other, value)
    return jnp.concatenate([low, high], axis=axis)


def body(tokens, norm_gain, qkv_weight, qk_gain, out_weight, layer_scale, tile_counts, owners):
    own_rows = tokens[0]
    chips = lax.axis_size("chip")
    cores = lax.axis_size("core")
    groups = chips * cores
    chip = lax.axis_index("chip")
    core = lax.axis_index("core")
    row_index = lax.axis_index("fsdp")
    row_count = lax.axis_size("fsdp")
    model_width = own_rows.shape[1]
    block = model_width // groups
    swap = [(0, 1), (1, 0)]
    spread = jnp.broadcast_to(out_weight[None], (row_count,) + out_weight.shape)
    head_rows = lax.all_to_all(spread, "fsdp", split_axis=0, concat_axis=0, tiled=True)
    per_row = out_weight.shape[1] // block
    head_rows = head_rows.reshape(row_count, HEAD_DIM, per_row, block).transpose(0, 2, 1, 3)
    weight_block = lax.all_to_all(
        head_rows.reshape(groups, HEAD_DIM, block),
        ("chip", "core"),
        split_axis=0,
        concat_axis=0,
        tiled=True,
    ).reshape(groups * HEAD_DIM, block)
    pair_weight = pair_up(weight_block, core, swap, 1)
    full_qkv = gather_blocks(qkv_weight, "fsdp", row_count)
    pair_qkv = pair_up(full_qkv, core, swap, 1)
    pair_qkv, pair_weight = lax.optimization_barrier((pair_qkv, pair_weight))
    pair_gain = pair_up(qk_gain, core, swap, 1).reshape(2, cores, HEAD_DIM)
    half = lax.all_gather(own_rows, "chip", axis=0, tiled=True)
    half_length = half.shape[0]
    piece = own_rows.shape[0]
    values = half.astype(jnp.float32)
    normed = (
        values * lax.rsqrt(jnp.mean(values * values, axis=-1, keepdims=True) + EPSILON) * norm_gain
    ).astype(jnp.bfloat16)
    projected = jnp.dot(normed, pair_qkv, preferred_element_type=jnp.float32)
    projected = projected.reshape(half_length, cores, 3, HEAD_DIM)
    queries = projected[:, :, 0]
    keys_part = projected[:, :, 1]
    values_part = projected[:, :, 2].astype(jnp.bfloat16)
    sums = gather_sum(
        jnp.stack(
            [jnp.sum(queries * queries, axis=(1, 2)), jnp.sum(keys_part * keys_part, axis=(1, 2))]
        ),
        "chip",
        chips,
    )
    window = groups * HEAD_DIM
    queries = (
        queries * lax.rsqrt(sums[0] / window + EPSILON)[:, None, None] * pair_gain[0][None]
    ).astype(jnp.bfloat16)
    keys_part = (
        keys_part * lax.rsqrt(sums[1] / window + EPSILON)[:, None, None] * pair_gain[1][None]
    ).astype(jnp.bfloat16)
    stacked = jnp.stack([queries, keys_part, values_part])
    mine = lax.dynamic_index_in_dim(stacked, core, axis=2, keepdims=False)
    theirs = lax.dynamic_index_in_dim(stacked, 1 - core, axis=2, keepdims=False)
    got = lax.ppermute(theirs, "core", swap)
    first_half = jnp.where(core == 0, mine, got).reshape(3, chips, piece, HEAD_DIM)
    second_half = jnp.where(core == 0, got, mine).reshape(3, chips, piece, HEAD_DIM)
    whole = jnp.stack([first_half, second_half], axis=2).reshape(3, groups * piece, HEAD_DIM)
    length = whole.shape[1]
    factor = HEAD_DIM ** (-0.5)
    covered = SLOTS * TILE
    tile_query = whole[0, :covered].reshape(SLOTS, TILE, HEAD_DIM)
    tile_key = whole[1, :covered].reshape(SLOTS, TILE, HEAD_DIM)
    tile_value = whole[2, :covered].reshape(SLOTS, TILE, HEAD_DIM)
    scores = (
        jnp.einsum("sqc,skc->sqk", tile_query, tile_key, preferred_element_type=jnp.float32)
        * factor
    )
    highest = jnp.max(scores, axis=-1, keepdims=True)
    exponent = jnp.exp(scores - highest)
    weights = (exponent / jnp.sum(exponent, axis=-1, keepdims=True)).astype(jnp.bfloat16)
    tile_out = jnp.einsum(
        "sqk,skc->sqc", weights, tile_value, preferred_element_type=jnp.float32
    ).astype(jnp.bfloat16)
    head_out = jnp.concatenate(
        [
            tile_out.reshape(covered, HEAD_DIM),
            jnp.zeros((length - covered, HEAD_DIM), jnp.bfloat16),
        ],
        axis=0,
    )
    by_half = head_out.reshape(chips, cores, piece, HEAD_DIM).transpose(1, 0, 2, 3)
    by_half = by_half.reshape(cores, half_length, HEAD_DIM)
    outgoing = jnp.broadcast_to(by_half[None], (chips, cores, half_length, HEAD_DIM))
    all_heads = lax.all_to_all(
        outgoing.reshape(groups, half_length, HEAD_DIM),
        ("chip", "core"),
        split_axis=0,
        concat_axis=0,
        tiled=True,
    )
    pair_tokens = lax.dynamic_slice_in_dim(half, chip * cores * block, cores * block, axis=1)
    pair_scale = lax.dynamic_slice_in_dim(layer_scale, chip * cores * block, cores * block)
    updated_half = head_sum(
        all_heads, pair_weight.reshape(groups, HEAD_DIM, cores * block), pair_tokens, pair_scale
    )
    keep = lax.dynamic_slice_in_dim(updated_half, core * block, block, axis=1)
    give = lax.dynamic_slice_in_dim(updated_half, (1 - core) * block, block, axis=1)
    taken = lax.ppermute(give, "core", swap)
    first_half = jnp.where(core == 0, keep, taken).reshape(chips, piece, block)
    second_half = jnp.where(core == 0, taken, keep).reshape(chips, piece, block)
    updated = jnp.stack([first_half, second_half], axis=1).reshape(length, block)
    patches = jnp.stack([updated[slot * TILE + 1 : (slot + 1) * TILE] for slot in range(SLOTS)])
    halves = GRID // 2
    square = patches.reshape(SLOTS, halves, 2, halves, 2, block).transpose(0, 1, 3, 5, 2, 4)
    merged = square.reshape(SLOTS, halves * halves, block * 4)
    holder, living = tile_owners(tile_counts, owners)
    own_holder = holder[row_index]
    own_living = living[row_index]
    destination = jnp.arange(row_count, dtype=jnp.int32)[:, None]
    sending = jnp.logical_and(destination == own_holder[None, :], own_living[None, :])
    outgoing = jnp.broadcast_to(merged[None], (row_count,) + merged.shape)
    received = lax.all_to_all(outgoing, "fsdp", split_axis=0, concat_axis=0, tiled=True)
    return place_tiles(received, holder, living, row_index)


def solution(mesh):
    fsdp_size = mesh.shape["fsdp"]
    dp_size = mesh.shape["dp"]
    split = Mesh(
        mesh.devices.reshape(fsdp_size, dp_size // 2, 2), ("fsdp", "chip", "core")
    )
    heads = ("chip", "core")
    placed = (
        P("fsdp", heads, None),
        P(),
        P("fsdp", heads),
        P(None, heads),
        P(heads, "fsdp"),
        P(),
        P(),
        P(),
    )
    return jax.shard_map(
        body, mesh=split, in_specs=placed, out_specs=P("fsdp", None, heads), check_vma=False
    )
```
